32 devices in a mesh: groups: 2 (over y), seq: 4 (over z), row: 2 (over x), col: 2 (over core).
Axes of the slice: x: 2, y: 2, z: 4, core: 2. Of those that a mesh axis runs over, the one named last changes fastest.
Arguments:
- acts: bfloat16 [3072, 4096], P(('groups', 'seq', 'row'), 'col'), parts along dimension 0, may hold values from -9 to 9
- w_query: bfloat16 [4096, 2048], P('seq', ('row', 'col')), may hold values from -0.1875 to 0.1875
- w_key: bfloat16 [4096, 2048], P('seq', ('row', 'col')), may hold values from -0.1875 to 0.1875
- w_value: bfloat16 [4096, 2048], P('seq', ('row', 'col')), may hold values from -0.09375 to 0.09375
Outputs:
- attended: bfloat16 [3072, 2048], P(('groups', 'seq'), ('row', 'col')), parts along dimension 0
The draws below stay inside these ranges and needn't reach their ends.
There are 2 independent parts, one for each index of `groups`. The reference program is written for one: setup_inputs(seed, part) draws one part's arguments, and reference() takes and returns one part's arrays. A program takes and returns all parts, laid end to end along the dimension named above; an argument that names none is the same for every part. Nothing has to cross between parts.
All inputs are finite; a program needn't handle non-finite values.
Results may differ from the reference program's by a relative error of at most 0.0055.
The reference program's roundings to bfloat16 on the way count: a program that leaves them out, or rounds other values in their place, can miss the bound.
Values may be sent and summed in bfloat16 or wider, within the bound.
No kernel may reach another device: no remote copies, remote signals or barrier semaphores. Data moves between devices by JAX's collectives and lax.ppermute only.
A program may use at most 64 MiB of HBM per device.

```python
import jax
import jax.numpy as jnp
from jax import lax

D = 4096
HEADS = 16
HD = 128
SPAN = 4
BLOCK = 384
TOKENS = 1536
N_SEQ = 4


def draw_acts(key, part):
    base_key = jax.random.fold_in(key, 0)
    values = jnp.clip(jax.random.normal(base_key, (TOKENS, D), jnp.float32), -6.0, 6.0)
    return values.astype(jnp.bfloat16)


def steps_of(rng, shape, pieces, smallest, high):
    gain = 1.0
    for axis_at, parts in pieces:
        steps = jax.random.uniform(jax.random.fold_in(jax.random.fold_in(rng, 6), axis_at), (parts,), jnp.float32, smallest / len(pieces), high / len(pieces))
        gain = gain * jnp.repeat(jnp.exp(steps), shape[axis_at] // parts).reshape((-1,) + (1,) * (len(shape) - 1 - axis_at))
    return gain


def gaussian(rng, shape, deviation, most, cuts=(), dtype=jnp.bfloat16):
    entries = deviation * jax.random.normal(rng, shape, jnp.float32)
    if cuts:
        entries = entries * steps_of(rng, shape, cuts, -0.22, 0.18)
    return jnp.clip(entries, -most, most).astype(dtype)


def setup_inputs(seed: int = 0, part: int = 0) -> dict:
    arg_keys = jax.random.split(jax.random.key(seed), 5)
    part_splits = jax.random.split(jax.random.fold_in(arg_keys[4], part), 5)
    acts = draw_acts(jax.random.fold_in(jax.random.fold_in(arg_keys[4], part), 71), part)
    w_query = gaussian(arg_keys[1], (D, HEADS * HD), (D // 4) ** -0.5, 0.1875, ((0, 4), (1, 4)))
    w_key = gaussian(arg_keys[2], (D, HEADS * HD), (D // 4) ** -0.5, 0.1875, ((0, 4), (1, 4)))
    w_value = gaussian(arg_keys[3], (D, HEADS * HD), D ** -0.5, 0.09375, ((0, 4), (1, 4)))
    return {"acts": acts, "w_query": w_query, "w_key": w_key, "w_value": w_value}


def reference(acts, w_query, w_key, w_value):
    inputs = acts.astype(jnp.float32)
    width = HEADS * HD

    def project(weight):
        product = jnp.dot(inputs, weight.astype(jnp.float32), precision=lax.Precision.HIGHEST)
        return product.astype(jnp.bfloat16).reshape(N_SEQ, BLOCK, HEADS, HD)
    query = project(w_query)
    keys = project(w_key)
    values = project(w_value)
    scale = 1.0 / jnp.sqrt(jnp.float32(HD))
    offsets = jnp.arange(SPAN).astype(jnp.int32)

    def one_block(index):
        picks = (index - offsets) % N_SEQ
        block_query = query[index].astype(jnp.float32)
        block_keys = keys[picks].reshape(SPAN * BLOCK, HEADS, HD).astype(jnp.float32)
        block_values = values[picks].reshape(SPAN * BLOCK, HEADS, HD).astype(jnp.float32)
        scores = jnp.einsum('qhd,khd->hqk', block_query, block_keys, precision=lax.Precision.HIGHEST) * scale
        top = lax.optimization_barrier(jnp.max(scores, axis=-1, keepdims=True))
        expos = jnp.exp(scores - top)
        total = lax.optimization_barrier(jnp.sum(expos, axis=-1))
        rounded = lax.optimization_barrier(expos.astype(jnp.bfloat16)).astype(jnp.float32)
        summed = jnp.einsum('hqk,khd->qhd', rounded, block_values, precision=lax.Precision.HIGHEST)
        return (summed / jnp.transpose(total)[:, :, None]).astype(jnp.bfloat16)
    result = lax.map(one_block, jnp.arange(N_SEQ).astype(jnp.int32))
    return result.reshape(TOKENS, width)
```

```python
import jax
import jax.numpy as jnp
from jax import lax
from jax.sharding import PartitionSpec as P

HD = 128
SPAN = 4


def passed_along(block, axis, distance):
    devices = range(lax.axis_size(axis))
    route = [((i - distance) % len(devices), i) for i in devices]
    return lax.ppermute(block, axis, route)


def swap_gather(piece, axis, dim):
    if lax.axis_size(axis) != 2:
        return lax.all_gather(piece, axis, axis=dim, tiled=True)
    first = lax.axis_index(axis) == 0
    other = lax.ppermute(piece, axis, [(0, 1), (1, 0)])
    low = jnp.where(first, piece, other)
    high = jnp.where(first, other, piece)
    return jnp.concatenate([low, high], axis=dim)


def full_columns(weight, shared):
    if not shared:
        return lax.all_gather(weight, "seq", axis=0, tiled=True)
    half = weight.shape[1] // 2
    own = lax.dynamic_slice_in_dim(weight, lax.axis_index("groups") * half, half, axis=1)
    own = lax.all_gather(own, "seq", axis=0, tiled=True)
    other = lax.ppermute(own, "groups", [(0, 1), (1, 0)])
    return jnp.concatenate([own, other], axis=1)


def per_device(acts, w_query, w_key, w_value):
    block = swap_gather(acts, "row", 0)
    block = swap_gather(block, "col", 1)
    tokens_here = block.shape[0]
    width = w_query.shape[1]
    heads_here = width // HD
    shared = lax.axis_size("groups") == 2 and width % (2 * HD) == 0
    pieces = tuple(full_columns(w, shared) for w in (w_key, w_value, w_query))
    key_sum, value_sum, query_sum = tuple(
        (jnp.dot(block, piece, preferred_element_type=jnp.float32) for piece in pieces)
    )
    query = query_sum.astype(jnp.bfloat16).reshape(tokens_here, heads_here, HD)
    packed = jnp.stack([key_sum.astype(jnp.bfloat16), value_sum.astype(jnp.bfloat16)])
    blocks_seen = [packed]
    current = packed
    for step in range(1, SPAN):
        current = passed_along(current, "seq", 1)
        blocks_seen.append(current)
    scale = 1.0 / jnp.sqrt(jnp.float32(HD))
    score_list = []
    for seen in blocks_seen:
        seen_keys = seen[0].reshape(-1, heads_here, HD)
        score_list.append(
            jnp.einsum("qhd,khd->hqk", query, seen_keys, preferred_element_type=jnp.float32) * scale
        )
    largest = score_list[0].max(axis=-1, keepdims=True)
    for scores in score_list[1:]:
        largest = jnp.maximum(largest, scores.max(axis=-1, keepdims=True))
    running_total = jnp.zeros((heads_here, tokens_here), jnp.float32)
    summed = jnp.zeros((tokens_here, heads_here, HD), jnp.float32)
    for scores, seen in zip(score_list, blocks_seen):
        expos = jnp.exp(scores - largest)
        running_total = running_total + jnp.sum(expos, axis=-1)
        seen_values = seen[1].reshape(-1, heads_here, HD)
        summed = summed + jnp.einsum(
            "hqk,khd->qhd",
            expos.astype(jnp.bfloat16),
            seen_values,
            preferred_element_type=jnp.float32,
        )
    attended = summed / jnp.transpose(running_total)[:, :, None]
    attended = attended.astype(jnp.bfloat16).reshape(tokens_here, width)
    if shared:
        attended = jnp.roll(attended, lax.axis_index("groups") * (width // 2), axis=1)
    return attended


def solution(mesh):
    in_specs = (
        P(("groups", "seq", "row"), "col"),
        P("seq", ("row", "col")),
        P("seq", ("row", "col")),
        P("seq", ("row", "col")),
    )
    out_specs = P(("groups", "seq"), ("row", "col"))
    return jax.shard_map(
        per_device, mesh=mesh, in_specs=in_specs, out_specs=out_specs, check_vma=False
    )
```

```python
import jax
import jax.numpy as jnp
from jax import lax
from jax.sharding import PartitionSpec as P

HD = 128
SPAN = 4


def passed_along(block, axis, distance):
    devices = range(lax.axis_size(axis))
    route = [((i - distance) % len(devices), i) for i in devices]
    return lax.ppermute(block, axis, route)


def swap_gather(piece, axis, dim):
    if lax.axis_size(axis) != 2:
        return lax.all_gather(piece, axis, axis=dim, tiled=True)
    first = lax.axis_index(axis) == 0
    other = lax.ppermute(piece, axis, [(0, 1), (1, 0)])
    low = jnp.where(first, piece, other)
    high = jnp.where(first, other, piece)
    return jnp.concatenate([low, high], axis=dim)


def full_columns(weight, shared):
    if not shared:
        return lax.all_gather(weight, "seq", axis=0, tiled=True)
    half = weight.shape[1] // 2
    own = lax.dynamic_slice_in_dim(weight, lax.axis_index("groups") * half, half, axis=1)
    own = lax.all_gather(own, "seq", axis=0, tiled=True)
    other = lax.ppermute(own, "groups", [(0, 1), (1, 0)])
    return jnp.concatenate([own, other], axis=1)


def per_device(acts, w_query, w_key, w_value):
    block = swap_gather(acts, "row", 0)
    block = swap_gather(block, "col", 1)
    tokens_here = block.shape[0]
    width = w_query.shape[1]
    heads_here = width // HD
    shared = lax.axis_size("groups") == 2 and width % (2 * HD) == 0
    pieces = tuple(full_columns(w, shared) for w in (w_key, w_value, w_query))
    key_sum, value_sum, query_sum = tuple(
        (jnp.dot(block, piece, preferred_element_type=jnp.float32) for piece in pieces)
    )
    query = query_sum.astype(jnp.bfloat16).reshape(tokens_here, heads_here, HD)
    packed = jnp.stack([key_sum.astype(jnp.bfloat16), value_sum.astype(jnp.bfloat16)])
    if lax.axis_size("seq") == SPAN:
        seen = lax.all_gather(packed, "seq", axis=1, tiled=True)
    else:
        blocks_seen = [packed]
        current = packed
        for step in range(1, SPAN):
            current = passed_along(current, "seq", 1)
            blocks_seen.append(current)
        seen = jnp.concatenate(blocks_seen, axis=1)
    seen_keys = seen[0].reshape(-1, heads_here, HD)
    seen_values = seen[1].reshape(-1, heads_here, HD)
    scale = 1.0 / jnp.sqrt(jnp.float32(HD))
    scores = jnp.einsum("qhd,khd->hqk", query, seen_keys, preferred_element_type=jnp.float32) * scale
    largest = scores.max(axis=-1, keepdims=True)
    expos = jnp.exp(scores - largest)
    running_total = jnp.sum(expos, axis=-1)
    summed = jnp.einsum(
        "hqk,khd->qhd", expos.astype(jnp.bfloat16), seen_values, preferred_element_type=jnp.float32
    )
    attended = summed / jnp.transpose(running_total)[:, :, None]
    attended = attended.astype(jnp.bfloat16).reshape(tokens_here, width)
    if shared:
        attended = jnp.roll(attended, lax.axis_index("groups") * (width // 2), axis=1)
    return attended


def solution(mesh):
    in_specs = (
        P(("groups", "seq", "row"), "col"),
        P("seq", ("row", "col")),
        P("seq", ("row", "col")),
        P("seq", ("row", "col")),
    )
    out_specs = P(("groups", "seq"), ("row", "col"))
    return jax.shard_map(
        per_device, mesh=mesh, in_specs=in_specs, out_specs=out_specs, check_vma=False
    )
```

```python
import jax
import jax.numpy as jnp
from jax import lax
from jax.sharding import PartitionSpec as P

HD = 128
SPAN = 4


def passed_along(block, axis, distance):
    devices = range(lax.axis_size(axis))
    route = [((i - distance) % len(devices), i) for i in devices]
    return lax.ppermute(block, axis, route)


def line_gather(piece):
    n = lax.axis_size("seq")
    here = lax.axis_index("seq")
    from_right = [piece]
    from_left = [piece]
    for k in range(1, n):
        from_right.append(lax.ppermute(from_right[-1], "seq", [(j, j - 1) for j in range(1, n - k + 1)]))
        from_left.append(lax.ppermute(from_left[-1], "seq", [(j, j + 1) for j in range(k - 1, n - 1)]))
    slots = [piece]
    for m in range(1, n):
        slots.append(jnp.where(here + m < n, from_right[m], from_left[n - m]))
    return jnp.concatenate(slots, axis=0)


def swap_gather(piece, axis, dim):
    if lax.axis_size(axis) != 2:
        return lax.all_gather(piece, axis, axis=dim, tiled=True)
    first = lax.axis_index(axis) == 0
    other = lax.ppermute(piece, axis, [(0, 1), (1, 0)])
    low = jnp.where(first, piece, other)
    high = jnp.where(first, other, piece)
    return jnp.concatenate([low, high], axis=dim)


def full_columns(weight, shared):
    if not shared:
        return lax.all_gather(weight, "seq", axis=0, tiled=True)
    half = weight.shape[1] // 2
    own = lax.dynamic_slice_in_dim(weight, lax.axis_index("groups") * half, half, axis=1)
    own = lax.all_gather(own, "seq", axis=0, tiled=True)
    other = lax.ppermute(own, "groups", [(0, 1), (1, 0)])
    return jnp.concatenate([own, other], axis=1)


def per_device(acts, w_query, w_key, w_value):
    block = swap_gather(acts, "row", 0)
    block = swap_gather(block, "col", 1)
    tokens_here = block.shape[0]
    width = w_query.shape[1]
    heads_here = width // HD
    shared = lax.axis_size("groups") == 2 and width % (2 * HD) == 0
    pieces = tuple(full_columns(w, shared) for w in (w_key, w_value, w_query))
    key_sum, value_sum, query_sum = tuple(
        (jnp.dot(block, piece, preferred_element_type=jnp.float32) for piece in pieces)
    )
    query = query_sum.astype(jnp.bfloat16).reshape(tokens_here, heads_here, HD)
    if lax.axis_size("seq") == SPAN:
        seen = jnp.stack(
            [line_gather(key_sum.astype(jnp.bfloat16)), line_gather(value_sum.astype(jnp.bfloat16))]
        )
    else:
        packed = jnp.stack([key_sum.astype(jnp.bfloat16), value_sum.astype(jnp.bfloat16)])
        blocks_seen = [packed]
        current = packed
        for step in range(1, SPAN):
            current = passed_along(current, "seq", 1)
            blocks_seen.append(current)
        seen = jnp.concatenate(blocks_seen, axis=1)
    seen_keys = seen[0].reshape(-1, heads_here, HD)
    seen_values = seen[1].reshape(-1, heads_here, HD)
    scale = 1.0 / jnp.sqrt(jnp.float32(HD))
    scores = jnp.einsum("qhd,khd->hqk", query, seen_keys, preferred_element_type=jnp.float32) * scale
    largest = scores.max(axis=-1, keepdims=True)
    expos = jnp.exp(scores - largest)
    running_total = jnp.sum(expos, axis=-1)
    summed = jnp.einsum(
        "hqk,khd->qhd", expos.astype(jnp.bfloat16), seen_values, preferred_element_type=jnp.float32
    )
    attended = summed / jnp.transpose(running_total)[:, :, None]
    attended = attended.astype(jnp.bfloat16).reshape(tokens_here, width)
    if shared:
        attended = jnp.roll(attended, lax.axis_index("groups") * (width // 2), axis=1)
    return attended


def solution(mesh):
    in_specs = (
        P(("groups", "seq", "row"), "col"),
        P("seq", ("row", "col")),
        P("seq", ("row", "col")),
        P("seq", ("row", "col")),
    )
    out_specs = P(("groups", "seq"), ("row", "col"))
    return jax.shard_map(
        per_device, mesh=mesh, in_specs=in_specs, out_specs=out_specs, check_vma=False
    )
```

```python
import jax
import jax.numpy as jnp
from jax import lax
from jax.sharding import PartitionSpec as P

HD = 128
SPAN = 4


def passed_along(block, axis, distance):
    devices = range(lax.axis_size(axis))
    route = [((i - distance) % len(devices), i) for i in devices]
    return lax.ppermute(block, axis, route)


def line_gather(piece):
    n = lax.axis_size("seq")
    here = lax.axis_index("seq")
    from_right = [piece]
    from_left = [piece]
    for k in range(1, n):
        from_right.append(lax.ppermute(from_right[-1], "seq", [(j, j - 1) for j in range(1, n - k + 1)]))
        from_left.append(lax.ppermute(from_left[-1], "seq", [(j, j + 1) for j in range(k - 1, n - 1)]))
    slots = [piece]
    for m in range(1, n):
        slots.append(jnp.where(here + m < n, from_right[m], from_left[n - m]))
    return jnp.concatenate(slots, axis=0)


def swap_gather(piece, axis, dim):
    if lax.axis_size(axis) != 2:
        return lax.all_gather(piece, axis, axis=dim, tiled=True)
    first = lax.axis_index(axis) == 0
    other = lax.ppermute(piece, axis, [(0, 1), (1, 0)])
    low = jnp.where(first, piece, other)
    high = jnp.where(first, other, piece)
    return jnp.concatenate([low, high], axis=dim)


def full_columns(weight, shared, after=None):
    if not shared:
        return lax.all_gather(weight, "seq", axis=0, tiled=True)
    rows, half = weight.shape[0], weight.shape[1] // 2
    group = lax.axis_index("groups")
    own = lax.dynamic_slice_in_dim(weight, group * half, half, axis=1)
    kept = lax.dynamic_slice_in_dim(weight, (1 - group) * half, half, axis=1)
    own = lax.all_gather(own, "seq", axis=0, tiled=True)
    own = jnp.roll(own, -lax.axis_index("seq") * rows, axis=0)
    if after is not None:
        own = lax.optimization_barrier((own, after))[0]
    other = lax.ppermute(own[rows:], "groups", [(0, 1), (1, 0)])
    return jnp.concatenate([own, jnp.concatenate([kept, other], axis=0)], axis=1)


def per_device(acts, w_query, w_key, w_value):
    block = swap_gather(acts, "row", 0)
    block = swap_gather(block, "col", 1)
    tokens_here = block.shape[0]
    width = w_query.shape[1]
    heads_here = width // HD
    shared = lax.axis_size("groups") == 2 and width % (2 * HD) == 0
    if shared:
        block = jnp.roll(block, -lax.axis_index("seq") * w_query.shape[0], axis=1)

    def project(weight, after=None):
        piece = full_columns(weight, shared, after)
        return jnp.dot(block, piece, preferred_element_type=jnp.float32).astype(jnp.bfloat16)

    key = project(w_key)
    value = project(w_value)
    query = project(w_query, key).reshape(tokens_here, heads_here, HD)
    if lax.axis_size("seq") == SPAN:
        seen = jnp.stack(
            [line_gather(key), line_gather(value)]
        )
    else:
        packed = jnp.stack([key, value])
        blocks_seen = [packed]
        current = packed
        for step in range(1, SPAN):
            current = passed_along(current, "seq", 1)
            blocks_seen.append(current)
        seen = jnp.concatenate(blocks_seen, axis=1)
    seen_keys = seen[0].reshape(-1, heads_here, HD)
    seen_values = seen[1].reshape(-1, heads_here, HD)
    scale = 1.0 / jnp.sqrt(jnp.float32(HD))
    scores = jnp.einsum("qhd,khd->hqk", query, seen_keys, preferred_element_type=jnp.float32) * scale
    largest = scores.max(axis=-1, keepdims=True)
    expos = jnp.exp(scores - largest)
    running_total = jnp.sum(expos, axis=-1)
    summed = jnp.einsum(
        "hqk,khd->qhd", expos.astype(jnp.bfloat16), seen_values, preferred_element_type=jnp.float32
    )
    attended = summed / jnp.transpose(running_total)[:, :, None]
    attended = attended.astype(jnp.bfloat16).reshape(tokens_here, width)
    if shared:
        attended = jnp.roll(attended, lax.axis_index("groups") * (width // 2), axis=1)
    return attended


def solution(mesh):
    in_specs = (
        P(("groups", "seq", "row"), "col"),
        P("seq", ("row", "col")),
        P("seq", ("row", "col")),
        P("seq", ("row", "col")),
    )
    out_specs = P(("groups", "seq"), ("row", "col"))
    return jax.shard_map(
        per_device, mesh=mesh, in_specs=in_specs, out_specs=out_specs, check_vma=False
    )
```

```python
import jax
import jax.numpy as jnp
from jax import lax
from jax.sharding import PartitionSpec as P

HD = 128
SPAN = 4


def passed_along(block, axis, distance):
    devices = range(lax.axis_size(axis))
    route = [((i - distance) % len(devices), i) for i in devices]
    return lax.ppermute(block, axis, route)


def line_gather(piece):
    n = lax.axis_size("seq")
    here = lax.axis_index("seq")
    from_right = [piece]
    from_left = [piece]
    for k in range(1, n):
        from_right.append(lax.ppermute(from_right[-1], "seq", [(j, j - 1) for j in range(1, n - k + 1)]))
        from_left.append(lax.ppermute(from_left[-1], "seq", [(j, j + 1) for j in range(k - 1, n - 1)]))
    slots = [piece]
    for m in range(1, n):
        slots.append(jnp.where(here + m < n, from_right[m], from_left[n - m]))
    return jnp.concatenate(slots, axis=0)


def swap_gather(piece, axis, dim):
    if lax.axis_size(axis) != 2:
        return lax.all_gather(piece, axis, axis=dim, tiled=True)
    first = lax.axis_index(axis) == 0
    other = lax.ppermute(piece, axis, [(0, 1), (1, 0)])
    low = jnp.where(first, piece, other)
    high = jnp.where(first, other, piece)
    return jnp.concatenate([low, high], axis=dim)


def column_chunks(weight, shared, after=None):
    if not shared:
        return [lax.all_gather(weight, "seq", axis=0, tiled=True)]
    rows, half = weight.shape[0], weight.shape[1] // 2
    group = lax.axis_index("groups")
    count = 2 if half % (2 * HD) == 0 else 1
    width = half // count
    owns, others = [], []
    for k in range(count):
        own = lax.dynamic_slice_in_dim(weight, group * half + k * width, width, axis=1)
        kept = lax.dynamic_slice_in_dim(weight, (1 - group) * half + k * width, width, axis=1)
        own = lax.all_gather(own, "seq", axis=0, tiled=True)
        own = jnp.roll(own, -lax.axis_index("seq") * rows, axis=0)
        if after is not None:
            own = lax.optimization_barrier((own, after))[0]
        other = lax.ppermute(own[rows:], "groups", [(0, 1), (1, 0)])
        owns.append(own)
        others.append(jnp.concatenate([kept, other], axis=0))
    return owns + others


def per_device(acts, w_query, w_key, w_value):
    block = swap_gather(acts, "row", 0)
    block = swap_gather(block, "col", 1)
    tokens_here = block.shape[0]
    width = w_query.shape[1]
    heads_here = width // HD
    shared = lax.axis_size("groups") == 2 and width % (2 * HD) == 0
    if shared:
        block = jnp.roll(block, -lax.axis_index("seq") * w_query.shape[0], axis=1)

    def project(weight, after=None):
        return jnp.concatenate(
            [
                jnp.dot(block, piece, preferred_element_type=jnp.float32).astype(jnp.bfloat16)
                for piece in column_chunks(weight, shared, after)
            ],
            axis=1,
        )

    key = project(w_key)
    value = project(w_value)
    query = project(w_query, key).reshape(tokens_here, heads_here, HD)
    if lax.axis_size("seq") == SPAN:
        seen = jnp.stack(
            [line_gather(key), line_gather(value)]
        )
    else:
        packed = jnp.stack([key, value])
        blocks_seen = [packed]
        current = packed
        for step in range(1, SPAN):
            current = passed_along(current, "seq", 1)
            blocks_seen.append(current)
        seen = jnp.concatenate(blocks_seen, axis=1)
    seen_keys = seen[0].reshape(-1, heads_here, HD)
    seen_values = seen[1].reshape(-1, heads_here, HD)
    scale = 1.0 / jnp.sqrt(jnp.float32(HD))
    scores = jnp.einsum("qhd,khd->hqk", query, seen_keys, preferred_element_type=jnp.float32) * scale
    largest = scores.max(axis=-1, keepdims=True)
    expos = jnp.exp(scores - largest)
    running_total = jnp.sum(expos, axis=-1)
    summed = jnp.einsum(
        "hqk,khd->qhd", expos.astype(jnp.bfloat16), seen_values, preferred_element_type=jnp.float32
    )
    attended = summed / jnp.transpose(running_total)[:, :, None]
    attended = attended.astype(jnp.bfloat16).reshape(tokens_here, width)
    if shared:
        attended = jnp.roll(attended, lax.axis_index("groups") * (width // 2), axis=1)
    return attended


def solution(mesh):
    in_specs = (
        P(("groups", "seq", "row"), "col"),
        P("seq", ("row", "col")),
        P("seq", ("row", "col")),
        P("seq", ("row", "col")),
    )
    out_specs = P(("groups", "seq"), ("row", "col"))
    return jax.shard_map(
        per_device, mesh=mesh, in_specs=in_specs, out_specs=out_specs, check_vma=False
    )
```

```python
import jax
import jax.numpy as jnp
from jax import lax
from jax.sharding import PartitionSpec as P

HD = 128
SPAN = 4


def passed_along(block, axis, distance):
    devices = range(lax.axis_size(axis))
    route = [((i - distance) % len(devices), i) for i in devices]
    return lax.ppermute(block, axis, route)


def line_gather(piece):
    n = lax.axis_size("seq")
    here = lax.axis_index("seq")
    from_right = [piece]
    from_left = [piece]
    for k in range(1, n):
        from_right.append(lax.ppermute(from_right[-1], "seq", [(j, j - 1) for j in range(1, n - k + 1)]))
        from_left.append(lax.ppermute(from_left[-1], "seq", [(j, j + 1) for j in range(k - 1, n - 1)]))
    slots = [piece]
    for m in range(1, n):
        slots.append(jnp.where(here + m < n, from_right[m], from_left[n - m]))
    return jnp.concatenate(slots, axis=0)


def swap_gather(piece, axis, dim):
    if lax.axis_size(axis) != 2:
        return lax.all_gather(piece, axis, axis=dim, tiled=True)
    first = lax.axis_index(axis) == 0
    other = lax.ppermute(piece, axis, [(0, 1), (1, 0)])
    low = jnp.where(first, piece, other)
    high = jnp.where(first, other, piece)
    return jnp.concatenate([low, high], axis=dim)


def full_columns(weight, shared, after=None):
    if not shared:
        return lax.all_gather(weight, "seq", axis=0, tiled=True)
    rows, half = weight.shape[0], weight.shape[1] // 2
    group = lax.axis_index("groups")
    own = lax.dynamic_slice_in_dim(weight, group * half, half, axis=1)
    kept = lax.dynamic_slice_in_dim(weight, (1 - group) * half, half, axis=1)
    own = lax.all_gather(own, "seq", axis=0, tiled=True)
    own = jnp.roll(own, -lax.axis_index("seq") * rows, axis=0)
    if after is not None:
        own = lax.optimization_barrier((own, after))[0]
    other = lax.ppermute(own[rows:], "groups", [(0, 1), (1, 0)])
    return jnp.concatenate([own, jnp.concatenate([kept, other], axis=0)], axis=1)


def per_device(acts, w_query, w_key, w_value):
    block = swap_gather(acts, "row", 0)
    block = swap_gather(block, "col", 1)
    tokens_here = block.shape[0]
    width = w_query.shape[1]
    heads_here = width // HD
    shared = lax.axis_size("groups") == 2 and width % (2 * HD) == 0
    if shared:
        block = jnp.roll(block, -lax.axis_index("seq") * w_query.shape[0], axis=1)

    def project(weight, after=None):
        piece = full_columns(weight, shared, after)
        return jnp.dot(block, piece, preferred_element_type=jnp.float32).astype(jnp.bfloat16)

    key = project(w_key)
    value = project(w_value)
    query = project(w_query, key).reshape(tokens_here, heads_here, HD)
    if lax.axis_size("seq") == SPAN:
        seen = jnp.stack(
            [line_gather(key), line_gather(value)]
        )
    else:
        packed = jnp.stack([key, value])
        blocks_seen = [packed]
        current = packed
        for step in range(1, SPAN):
            current = passed_along(current, "seq", 1)
            blocks_seen.append(current)
        seen = jnp.concatenate(blocks_seen, axis=1)
    seen_keys = seen[0].reshape(-1, heads_here, HD)
    seen_values = seen[1].reshape(-1, heads_here, HD)
    scale = 1.0 / jnp.sqrt(jnp.float32(HD))
    scores = jnp.einsum("qhd,khd->hqk", query, seen_keys, preferred_element_type=jnp.float32) * scale
    largest = scores.max(axis=-1, keepdims=True)
    expos = jnp.exp(scores - largest)
    running_total = jnp.sum(expos, axis=-1)
    summed = jnp.einsum(
        "hqk,khd->qhd", expos.astype(jnp.bfloat16), seen_values, preferred_element_type=jnp.float32
    )
    attended = summed / jnp.transpose(running_total)[:, :, None]
    attended = attended.astype(jnp.bfloat16).reshape(tokens_here, width)
    if shared:
        attended = jnp.roll(attended, lax.axis_index("groups") * (width // 2), axis=1)
    return attended


def to_workers(piece):
    near = lax.ppermute(piece, "seq", [(0, 1), (3, 2)])
    across = lax.ppermute(piece, "seq", [(1, 2), (2, 1)])
    far = lax.ppermute(near, "seq", [(1, 2), (2, 1)])
    return [piece, near, across, far]


def worker_columns(weight, after=None):
    rows, half = weight.shape[0], weight.shape[1] // 2
    group = lax.axis_index("groups")
    own = lax.dynamic_slice_in_dim(weight, group * half, half, axis=1)
    kept = lax.dynamic_slice_in_dim(weight, (1 - group) * half, half, axis=1)
    foreign = jnp.concatenate(to_workers(own)[1:], axis=0)
    if after is not None:
        foreign = lax.optimization_barrier((foreign, after))[0]
    other = lax.ppermute(foreign, "groups", [(0, 1), (1, 0)])
    return jnp.concatenate(
        [jnp.concatenate([own, foreign], axis=0), jnp.concatenate([kept, other], axis=0)], axis=1
    )


def paired_per_device(acts, w_query, w_key, w_value):
    here = lax.axis_index("seq")
    worker = (here == 1) | (here == 2)
    near = jnp.where(here == 1, 0, 3)
    order = [here, near, 3 - here, 3 - near]
    both = jnp.stack([acts, lax.ppermute(acts, "seq", [(0, 1), (3, 2)])])
    both = swap_gather(both, "row", 1)
    both = swap_gather(both, "col", 2)
    tokens = both.reshape(-1, both.shape[2])
    rows = w_query.shape[0]
    tokens = jnp.concatenate(
        [lax.dynamic_slice_in_dim(tokens, index * rows, rows, axis=1) for index in order], axis=1
    )
    tokens_here = tokens.shape[0]
    width = w_query.shape[1]
    heads_here = width // HD

    def project(weight, after=None):
        piece = worker_columns(weight, after)
        return jnp.dot(tokens, piece, preferred_element_type=jnp.float32).astype(jnp.bfloat16)

    key = project(w_key)
    value = project(w_value)
    query = project(w_query, key).reshape(tokens_here, heads_here, HD)
    packed = jnp.stack([key, value])
    seen = jnp.concatenate([packed, lax.ppermute(packed, "seq", [(1, 2), (2, 1)])], axis=1)
    seen_keys = seen[0].reshape(-1, heads_here, HD)
    seen_values = seen[1].reshape(-1, heads_here, HD)
    scale = 1.0 / jnp.sqrt(jnp.float32(HD))
    scores = jnp.einsum("qhd,khd->hqk", query, seen_keys, preferred_element_type=jnp.float32) * scale
    largest = scores.max(axis=-1, keepdims=True)
    expos = jnp.exp(scores - largest)
    running_total = jnp.sum(expos, axis=-1)
    summed = jnp.einsum(
        "hqk,khd->qhd", expos.astype(jnp.bfloat16), seen_values, preferred_element_type=jnp.float32
    )
    attended = summed / jnp.transpose(running_total)[:, :, None]
    attended = attended.astype(jnp.bfloat16).reshape(tokens_here, width)
    attended = jnp.roll(attended, lax.axis_index("groups") * (width // 2), axis=1)
    block = tokens_here // 2
    back = lax.ppermute(attended[block:], "seq", [(1, 0), (2, 3)])
    return jnp.where(worker, attended[:block], back)


def chosen(acts, w_query, w_key, w_value):
    width = w_query.shape[1]
    if (
        lax.axis_size("seq") == 4
        and SPAN == 4
        and lax.axis_size("groups") == 2
        and width % (2 * HD) == 0
    ):
        return paired_per_device(acts, w_query, w_key, w_value)
    return per_device(acts, w_query, w_key, w_value)


def solution(mesh):
    in_specs = (
        P(("groups", "seq", "row"), "col"),
        P("seq", ("row", "col")),
        P("seq", ("row", "col")),
        P("seq", ("row", "col")),
    )
    out_specs = P(("groups", "seq"), ("row", "col"))
    return jax.shard_map(
        chosen, mesh=mesh, in_specs=in_specs, out_specs=out_specs, check_vma=False
    )
```

```python
import jax
import jax.numpy as jnp
from jax import lax
from jax.sharding import PartitionSpec as P

HD = 128
SPAN = 4


def passed_along(block, axis, distance):
    devices = range(lax.axis_size(axis))
    route = [((i - distance) % len(devices), i) for i in devices]
    return lax.ppermute(block, axis, route)


def line_gather(piece):
    n = lax.axis_size("seq")
    here = lax.axis_index("seq")
    from_right = [piece]
    from_left = [piece]
    for k in range(1, n):
        from_right.append(lax.ppermute(from_right[-1], "seq", [(j, j - 1) for j in range(1, n - k + 1)]))
        from_left.append(lax.ppermute(from_left[-1], "seq", [(j, j + 1) for j in range(k - 1, n - 1)]))
    slots = [piece]
    for m in range(1, n):
        slots.append(jnp.where(here + m < n, from_right[m], from_left[n - m]))
    return jnp.concatenate(slots, axis=0)


def swap_gather(piece, axis, dim):
    if lax.axis_size(axis) != 2:
        return lax.all_gather(piece, axis, axis=dim, tiled=True)
    first = lax.axis_index(axis) == 0
    other = lax.ppermute(piece, axis, [(0, 1), (1, 0)])
    low = jnp.where(first, piece, other)
    high = jnp.where(first, other, piece)
    return jnp.concatenate([low, high], axis=dim)


def full_columns(weight, shared, after=None):
    if not shared:
        return lax.all_gather(weight, "seq", axis=0, tiled=True)
    rows, half = weight.shape[0], weight.shape[1] // 2
    group = lax.axis_index("groups")
    own = lax.dynamic_slice_in_dim(weight, group * half, half, axis=1)
    kept = lax.dynamic_slice_in_dim(weight, (1 - group) * half, half, axis=1)
    if after is None:
        own = lax.all_gather(own, "seq", axis=0, tiled=True)
        own = jnp.roll(own, -lax.axis_index("seq") * rows, axis=0)
        other = lax.ppermute(own[rows:], "groups", [(0, 1), (1, 0)])
    else:
        own = line_gather(own) if lax.axis_size("seq") == SPAN else jnp.roll(
            lax.all_gather(own, "seq", axis=0, tiled=True), -lax.axis_index("seq") * rows, axis=0
        )
        foreign = lax.optimization_barrier((own[rows:], after))[0]
        both = lax.all_gather(foreign, "groups", axis=0, tiled=False)
        other = both[1 - group]
    return jnp.concatenate([own, jnp.concatenate([kept, other], axis=0)], axis=1)


def per_device(acts, w_query, w_key, w_value):
    block = swap_gather(acts, "row", 0)
    block = swap_gather(block, "col", 1)
    tokens_here = block.shape[0]
    width = w_query.shape[1]
    heads_here = width // HD
    shared = lax.axis_size("groups") == 2 and width % (2 * HD) == 0
    if shared:
        block = jnp.roll(block, -lax.axis_index("seq") * w_query.shape[0], axis=1)

    def project(weight, after=None):
        piece = full_columns(weight, shared, after)
        return jnp.dot(block, piece, preferred_element_type=jnp.float32).astype(jnp.bfloat16)

    key = project(w_key)
    value = project(w_value)
    query = project(w_query, key).reshape(tokens_here, heads_here, HD)
    if lax.axis_size("seq") == SPAN:
        seen = jnp.stack(
            [line_gather(key), line_gather(value)]
        )
    else:
        packed = jnp.stack([key, value])
        blocks_seen = [packed]
        current = packed
        for step in range(1, SPAN):
            current = passed_along(current, "seq", 1)
            blocks_seen.append(current)
        seen = jnp.concatenate(blocks_seen, axis=1)
    seen_keys = seen[0].reshape(-1, heads_here, HD)
    seen_values = seen[1].reshape(-1, heads_here, HD)
    scale = 1.0 / jnp.sqrt(jnp.float32(HD))
    scores = jnp.einsum("qhd,khd->hqk", query, seen_keys, preferred_element_type=jnp.float32) * scale
    largest = scores.max(axis=-1, keepdims=True)
    expos = jnp.exp(scores - largest)
    running_total = jnp.sum(expos, axis=-1)
    summed = jnp.einsum(
        "hqk,khd->qhd", expos.astype(jnp.bfloat16), seen_values, preferred_element_type=jnp.float32
    )
    attended = summed / jnp.transpose(running_total)[:, :, None]
    attended = attended.astype(jnp.bfloat16).reshape(tokens_here, width)
    if shared:
        attended = jnp.roll(attended, lax.axis_index("groups") * (width // 2), axis=1)
    return attended


def solution(mesh):
    in_specs = (
        P(("groups", "seq", "row"), "col"),
        P("seq", ("row", "col")),
        P("seq", ("row", "col")),
        P("seq", ("row", "col")),
    )
    out_specs = P(("groups", "seq"), ("row", "col"))
    return jax.shard_map(
        per_device, mesh=mesh, in_specs=in_specs, out_specs=out_specs, check_vma=False
    )
```

```python
import jax
import jax.numpy as jnp
from jax import lax
from jax.sharding import PartitionSpec as P

HD = 128
SPAN = 4


def passed_along(block, axis, distance):
    devices = range(lax.axis_size(axis))
    route = [((i - distance) % len(devices), i) for i in devices]
    return lax.ppermute(block, axis, route)


def line_gather(piece):
    n = lax.axis_size("seq")
    here = lax.axis_index("seq")
    from_right = [piece]
    from_left = [piece]
    for k in range(1, n):
        from_right.append(lax.ppermute(from_right[-1], "seq", [(j, j - 1) for j in range(1, n - k + 1)]))
        from_left.append(lax.ppermute(from_left[-1], "seq", [(j, j + 1) for j in range(k - 1, n - 1)]))
    slots = [piece]
    for m in range(1, n):
        slots.append(jnp.where(here + m < n, from_right[m], from_left[n - m]))
    return jnp.concatenate(slots, axis=0)


def swap_gather(piece, axis, dim):
    if lax.axis_size(axis) != 2:
        return lax.all_gather(piece, axis, axis=dim, tiled=True)
    first = lax.axis_index(axis) == 0
    other = lax.ppermute(piece, axis, [(0, 1), (1, 0)])
    low = jnp.where(first, piece, other)
    high = jnp.where(first, other, piece)
    return jnp.concatenate([low, high], axis=dim)


def full_columns(weight, shared, after=None):
    if not shared:
        return [lax.all_gather(weight, "seq", axis=0, tiled=True)]
    rows, half = weight.shape[0], weight.shape[1] // 2
    group = lax.axis_index("groups")
    own = lax.dynamic_slice_in_dim(weight, group * half, half, axis=1)
    kept = lax.dynamic_slice_in_dim(weight, (1 - group) * half, half, axis=1)
    own = lax.all_gather(own, "seq", axis=0, tiled=True)
    own = jnp.roll(own, -lax.axis_index("seq") * rows, axis=0)
    if after is not None:
        own = lax.optimization_barrier((own, after))[0]
    other = lax.ppermute(own[rows:], "groups", [(0, 1), (1, 0)])
    return [own, jnp.concatenate([kept, other], axis=0)]


def per_device(acts, w_query, w_key, w_value):
    block = swap_gather(acts, "row", 0)
    block = swap_gather(block, "col", 1)
    tokens_here = block.shape[0]
    width = w_query.shape[1]
    heads_here = width // HD
    shared = lax.axis_size("groups") == 2 and width % (2 * HD) == 0
    if shared:
        block = jnp.roll(block, -lax.axis_index("seq") * w_query.shape[0], axis=1)

    def project(weight, after=None):
        return [
            jnp.dot(block, piece, preferred_element_type=jnp.float32).astype(jnp.bfloat16)
            for piece in full_columns(weight, shared, after)
        ]

    key = jnp.concatenate(project(w_key), axis=1)
    value = jnp.concatenate(project(w_value), axis=1)
    queries = project(w_query, key)
    if lax.axis_size("seq") == SPAN:
        seen = jnp.stack([line_gather(key), line_gather(value)])
    else:
        packed = jnp.stack([key, value])
        blocks_seen = [packed]
        current = packed
        for step in range(1, SPAN):
            current = passed_along(current, "seq", 1)
            blocks_seen.append(current)
        seen = jnp.concatenate(blocks_seen, axis=1)
    seen_keys = seen[0].reshape(-1, heads_here, HD)
    seen_values = seen[1].reshape(-1, heads_here, HD)
    scale = 1.0 / jnp.sqrt(jnp.float32(HD))
    outputs = []
    first = 0
    for query in queries:
        count = query.shape[1] // HD
        query = query.reshape(tokens_here, count, HD)
        part_keys = seen_keys[:, first : first + count]
        part_values = seen_values[:, first : first + count]
        first += count
        scores = jnp.einsum("qhd,khd->hqk", query, part_keys, preferred_element_type=jnp.float32) * scale
        largest = scores.max(axis=-1, keepdims=True)
        expos = jnp.exp(scores - largest)
        running_total = jnp.sum(expos, axis=-1)
        summed = jnp.einsum(
            "hqk,khd->qhd", expos.astype(jnp.bfloat16), part_values, preferred_element_type=jnp.float32
        )
        attended = summed / jnp.transpose(running_total)[:, :, None]
        outputs.append(attended.astype(jnp.bfloat16).reshape(tokens_here, count * HD))
    attended = jnp.concatenate(outputs, axis=1)
    if shared:
        attended = jnp.roll(attended, lax.axis_index("groups") * (width // 2), axis=1)
    return attended


def solution(mesh):
    in_specs = (
        P(("groups", "seq", "row"), "col"),
        P("seq", ("row", "col")),
        P("seq", ("row", "col")),
        P("seq", ("row", "col")),
    )
    out_specs = P(("groups", "seq"), ("row", "col"))
    return jax.shard_map(
        per_device, mesh=mesh, in_specs=in_specs, out_specs=out_specs, check_vma=False
    )
```

```python
import jax
import jax.numpy as jnp
from jax import lax
from jax.sharding import PartitionSpec as P

HD = 128
SPAN = 4


def passed_along(block, axis, distance):
    devices = range(lax.axis_size(axis))
    route = [((i - distance) % len(devices), i) for i in devices]
    return lax.ppermute(block, axis, route)


def line_gather(piece):
    n = lax.axis_size("seq")
    here = lax.axis_index("seq")
    from_right = [piece]
    from_left = [piece]
    for k in range(1, n):
        from_right.append(lax.ppermute(from_right[-1], "seq", [(j, j - 1) for j in range(1, n - k + 1)]))
        from_left.append(lax.ppermute(from_left[-1], "seq", [(j, j + 1) for j in range(k - 1, n - 1)]))
    slots = [piece]
    for m in range(1, n):
        slots.append(jnp.where(here + m < n, from_right[m], from_left[n - m]))
    return jnp.concatenate(slots, axis=0)


def swap_gather(piece, axis, dim):
    if lax.axis_size(axis) != 2:
        return lax.all_gather(piece, axis, axis=dim, tiled=True)
    first = lax.axis_index(axis) == 0
    other = lax.ppermute(piece, axis, [(0, 1), (1, 0)])
    low = jnp.where(first, piece, other)
    high = jnp.where(first, other, piece)
    return jnp.concatenate([low, high], axis=dim)


def full_columns(weight, shared, after=None):
    if not shared:
        return [lax.all_gather(weight, "seq", axis=0, tiled=True)]
    rows, half = weight.shape[0], weight.shape[1] // 2
    group = lax.axis_index("groups")
    own = lax.dynamic_slice_in_dim(weight, group * half, half, axis=1)
    kept = lax.dynamic_slice_in_dim(weight, (1 - group) * half, half, axis=1)
    if lax.axis_size("seq") == SPAN:
        own = line_gather(own)
    else:
        own = lax.all_gather(own, "seq", axis=0, tiled=True)
        own = jnp.roll(own, -lax.axis_index("seq") * rows, axis=0)
    if after is not None:
        own = lax.optimization_barrier((own, after))[0]
    other = lax.ppermute(own[rows:], "groups", [(0, 1), (1, 0)])
    return [own, jnp.concatenate([kept, other], axis=0)]


def per_device(acts, w_query, w_key, w_value):
    block = swap_gather(acts, "row", 0)
    block = swap_gather(block, "col", 1)
    tokens_here = block.shape[0]
    width = w_query.shape[1]
    heads_here = width // HD
    shared = lax.axis_size("groups") == 2 and width % (2 * HD) == 0
    if shared:
        block = jnp.roll(block, -lax.axis_index("seq") * w_query.shape[0], axis=1)

    def project(weight, after=None):
        return [
            jnp.dot(block, piece, preferred_element_type=jnp.float32).astype(jnp.bfloat16)
            for piece in full_columns(weight, shared, after)
        ]

    key = jnp.concatenate(project(w_key), axis=1)
    value = jnp.concatenate(project(w_value), axis=1)
    queries = project(w_query, key)
    if lax.axis_size("seq") == SPAN:
        seen = jnp.stack([line_gather(key), line_gather(value)])
    else:
        packed = jnp.stack([key, value])
        blocks_seen = [packed]
        current = packed
        for step in range(1, SPAN):
            current = passed_along(current, "seq", 1)
            blocks_seen.append(current)
        seen = jnp.concatenate(blocks_seen, axis=1)
    seen_keys = seen[0].reshape(-1, heads_here, HD)
    seen_values = seen[1].reshape(-1, heads_here, HD)
    scale = 1.0 / jnp.sqrt(jnp.float32(HD))
    outputs = []
    first = 0
    for query in queries:
        count = query.shape[1] // HD
        query = query.reshape(tokens_here, count, HD)
        part_keys = seen_keys[:, first : first + count]
        part_values = seen_values[:, first : first + count]
        first += count
        scores = jnp.einsum("qhd,khd->hqk", query, part_keys, preferred_element_type=jnp.float32) * scale
        largest = scores.max(axis=-1, keepdims=True)
        expos = jnp.exp(scores - largest)
        running_total = jnp.sum(expos, axis=-1)
        summed = jnp.einsum(
            "hqk,khd->qhd", expos.astype(jnp.bfloat16), part_values, preferred_element_type=jnp.float32
        )
        attended = summed / jnp.transpose(running_total)[:, :, None]
        outputs.append(attended.astype(jnp.bfloat16).reshape(tokens_here, count * HD))
    attended = jnp.concatenate(outputs, axis=1)
    if shared:
        attended = jnp.roll(attended, lax.axis_index("groups") * (width // 2), axis=1)
    return attended


def solution(mesh):
    in_specs = (
        P(("groups", "seq", "row"), "col"),
        P("seq", ("row", "col")),
        P("seq", ("row", "col")),
        P("seq", ("row", "col")),
    )
    out_specs = P(("groups", "seq"), ("row", "col"))
    return jax.shard_map(
        per_device, mesh=mesh, in_specs=in_specs, out_specs=out_specs, check_vma=False
    )
```

```python
import jax
import jax.numpy as jnp
from jax import lax
from jax.sharding import PartitionSpec as P

HD = 128
SPAN = 4


def passed_along(block, axis, distance):
    devices = range(lax.axis_size(axis))
    route = [((i - distance) % len(devices), i) for i in devices]
    return lax.ppermute(block, axis, route)


def line_gather(piece):
    n = lax.axis_size("seq")
    here = lax.axis_index("seq")
    from_right = [piece]
    from_left = [piece]
    for k in range(1, n):
        from_right.append(lax.ppermute(from_right[-1], "seq", [(j, j - 1) for j in range(1, n - k + 1)]))
        from_left.append(lax.ppermute(from_left[-1], "seq", [(j, j + 1) for j in range(k - 1, n - 1)]))
    slots = [piece]
    for m in range(1, n):
        slots.append(jnp.where(here + m < n, from_right[m], from_left[n - m]))
    return jnp.concatenate(slots, axis=0)


def swap_gather(piece, axis, dim):
    if lax.axis_size(axis) != 2:
        return lax.all_gather(piece, axis, axis=dim, tiled=True)
    first = lax.axis_index(axis) == 0
    other = lax.ppermute(piece, axis, [(0, 1), (1, 0)])
    low = jnp.where(first, piece, other)
    high = jnp.where(first, other, piece)
    return jnp.concatenate([low, high], axis=dim)


def full_columns(weight, shared, after=None):
    if not shared:
        return [lax.all_gather(weight, "seq", axis=0, tiled=True)]
    rows, half = weight.shape[0], weight.shape[1] // 2
    group = lax.axis_index("groups")
    own = lax.dynamic_slice_in_dim(weight, group * half, half, axis=1)
    kept = lax.dynamic_slice_in_dim(weight, (1 - group) * half, half, axis=1)
    own = lax.all_gather(own, "seq", axis=0, tiled=True)
    own = jnp.roll(own, -lax.axis_index("seq") * rows, axis=0)
    if after is not None:
        own = lax.optimization_barrier((own, after))[0]
    other = lax.ppermute(own[rows:], "groups", [(0, 1), (1, 0)])
    return [own, (kept, other)]


def per_device(acts, w_query, w_key, w_value):
    block = swap_gather(acts, "row", 0)
    block = swap_gather(block, "col", 1)
    tokens_here = block.shape[0]
    width = w_query.shape[1]
    heads_here = width // HD
    shared = lax.axis_size("groups") == 2 and width % (2 * HD) == 0
    if shared:
        block = jnp.roll(block, -lax.axis_index("seq") * w_query.shape[0], axis=1)

    def product(piece):
        if isinstance(piece, tuple):
            kept, other = piece
            rows = kept.shape[0]
            early = jnp.dot(block[:, :rows], kept, preferred_element_type=jnp.float32)
            return early + jnp.dot(block[:, rows:], other, preferred_element_type=jnp.float32)
        return jnp.dot(block, piece, preferred_element_type=jnp.float32)

    def project(weight, after=None):
        return [product(piece).astype(jnp.bfloat16) for piece in full_columns(weight, shared, after)]

    key = jnp.concatenate(project(w_key), axis=1)
    value = jnp.concatenate(project(w_value), axis=1)
    queries = project(w_query, key)
    if lax.axis_size("seq") == SPAN:
        seen = jnp.stack([line_gather(key), line_gather(value)])
    else:
        packed = jnp.stack([key, value])
        blocks_seen = [packed]
        current = packed
        for step in range(1, SPAN):
            current = passed_along(current, "seq", 1)
            blocks_seen.append(current)
        seen = jnp.concatenate(blocks_seen, axis=1)
    seen_keys = seen[0].reshape(-1, heads_here, HD)
    seen_values = seen[1].reshape(-1, heads_here, HD)
    scale = 1.0 / jnp.sqrt(jnp.float32(HD))
    outputs = []
    first = 0
    for query in queries:
        count = query.shape[1] // HD
        query = query.reshape(tokens_here, count, HD)
        part_keys = seen_keys[:, first : first + count]
        part_values = seen_values[:, first : first + count]
        first += count
        scores = jnp.einsum("qhd,khd->hqk", query, part_keys, preferred_element_type=jnp.float32) * scale
        largest = scores.max(axis=-1, keepdims=True)
        expos = jnp.exp(scores - largest)
        running_total = jnp.sum(expos, axis=-1)
        summed = jnp.einsum(
            "hqk,khd->qhd", expos.astype(jnp.bfloat16), part_values, preferred_element_type=jnp.float32
        )
        attended = summed / jnp.transpose(running_total)[:, :, None]
        outputs.append(attended.astype(jnp.bfloat16).reshape(tokens_here, count * HD))
    attended = jnp.concatenate(outputs, axis=1)
    if shared:
        attended = jnp.roll(attended, lax.axis_index("groups") * (width // 2), axis=1)
    return attended


def solution(mesh):
    in_specs = (
        P(("groups", "seq", "row"), "col"),
        P("seq", ("row", "col")),
        P("seq", ("row", "col")),
        P("seq", ("row", "col")),
    )
    out_specs = P(("groups", "seq"), ("row", "col"))
    return jax.shard_map(
        per_device, mesh=mesh, in_specs=in_specs, out_specs=out_specs, check_vma=False
    )
```

```python
import jax
import jax.numpy as jnp
from jax import lax
from jax.sharding import PartitionSpec as P

HD = 128
SPAN = 4


def passed_along(block, axis, distance):
    devices = range(lax.axis_size(axis))
    route = [((i - distance) % len(devices), i) for i in devices]
    return lax.ppermute(block, axis, route)


def line_gather(piece):
    n = lax.axis_size("seq")
    here = lax.axis_index("seq")
    from_right = [piece]
    from_left = [piece]
    for k in range(1, n):
        from_right.append(lax.ppermute(from_right[-1], "seq", [(j, j - 1) for j in range(1, n - k + 1)]))
        from_left.append(lax.ppermute(from_left[-1], "seq", [(j, j + 1) for j in range(k - 1, n - 1)]))
    slots = [piece]
    for m in range(1, n):
        slots.append(jnp.where(here + m < n, from_right[m], from_left[n - m]))
    return jnp.concatenate(slots, axis=0)


def swap_gather(piece, axis, dim):
    if lax.axis_size(axis) != 2:
        return lax.all_gather(piece, axis, axis=dim, tiled=True)
    first = lax.axis_index(axis) == 0
    other = lax.ppermute(piece, axis, [(0, 1), (1, 0)])
    low = jnp.where(first, piece, other)
    high = jnp.where(first, other, piece)
    return jnp.concatenate([low, high], axis=dim)


def full_columns(weight, shared, after=None):
    if not shared:
        return [lax.all_gather(weight, "seq", axis=0, tiled=True)]
    rows, half = weight.shape[0], weight.shape[1] // 2
    group = lax.axis_index("groups")
    own = lax.dynamic_slice_in_dim(weight, group * half, half, axis=1)
    kept = lax.dynamic_slice_in_dim(weight, (1 - group) * half, half, axis=1)
    own = lax.all_gather(own, "seq", axis=0, tiled=True)
    own = jnp.roll(own, -lax.axis_index("seq") * rows, axis=0)
    if after is not None:
        own = lax.optimization_barrier((own, after))[0]
    split = rows + (own.shape[0] - rows) // 2
    first = lax.ppermute(own[rows:split], "groups", [(0, 1), (1, 0)])
    second = lax.ppermute(own[split:], "groups", [(0, 1), (1, 0)])
    return [own, jnp.concatenate([kept, first, second], axis=0)]


def per_device(acts, w_query, w_key, w_value):
    block = swap_gather(acts, "row", 0)
    block = swap_gather(block, "col", 1)
    tokens_here = block.shape[0]
    width = w_query.shape[1]
    heads_here = width // HD
    shared = lax.axis_size("groups") == 2 and width % (2 * HD) == 0
    if shared:
        block = jnp.roll(block, -lax.axis_index("seq") * w_query.shape[0], axis=1)

    def project(weight, after=None):
        return [
            jnp.dot(block, piece, preferred_element_type=jnp.float32).astype(jnp.bfloat16)
            for piece in full_columns(weight, shared, after)
        ]

    key = jnp.concatenate(project(w_key), axis=1)
    value = jnp.concatenate(project(w_value), axis=1)
    queries = project(w_query, key)
    if lax.axis_size("seq") == SPAN:
        seen = jnp.stack([line_gather(key), line_gather(value)])
    else:
        packed = jnp.stack([key, value])
        blocks_seen = [packed]
        current = packed
        for step in range(1, SPAN):
            current = passed_along(current, "seq", 1)
            blocks_seen.append(current)
        seen = jnp.concatenate(blocks_seen, axis=1)
    seen_keys = seen[0].reshape(-1, heads_here, HD)
    seen_values = seen[1].reshape(-1, heads_here, HD)
    scale = 1.0 / jnp.sqrt(jnp.float32(HD))
    outputs = []
    first = 0
    for query in queries:
        count = query.shape[1] // HD
        query = query.reshape(tokens_here, count, HD)
        part_keys = seen_keys[:, first : first + count]
        part_values = seen_values[:, first : first + count]
        first += count
        scores = jnp.einsum("qhd,khd->hqk", query, part_keys, preferred_element_type=jnp.float32) * scale
        largest = scores.max(axis=-1, keepdims=True)
        expos = jnp.exp(scores - largest)
        running_total = jnp.sum(expos, axis=-1)
        summed = jnp.einsum(
            "hqk,khd->qhd", expos.astype(jnp.bfloat16), part_values, preferred_element_type=jnp.float32
        )
        attended = summed / jnp.transpose(running_total)[:, :, None]
        outputs.append(attended.astype(jnp.bfloat16).reshape(tokens_here, count * HD))
    attended = jnp.concatenate(outputs, axis=1)
    if shared:
        attended = jnp.roll(attended, lax.axis_index("groups") * (width // 2), axis=1)
    return attended


def solution(mesh):
    in_specs = (
        P(("groups", "seq", "row"), "col"),
        P("seq", ("row", "col")),
        P("seq", ("row", "col")),
        P("seq", ("row", "col")),
    )
    out_specs = P(("groups", "seq"), ("row", "col"))
    return jax.shard_map(
        per_device, mesh=mesh, in_specs=in_specs, out_specs=out_specs, check_vma=False
    )
```

```python
import jax
import jax.numpy as jnp
from jax import lax
from jax.sharding import PartitionSpec as P

HD = 128
SPAN = 4


def passed_along(block, axis, distance):
    devices = range(lax.axis_size(axis))
    route = [((i - distance) % len(devices), i) for i in devices]
    return lax.ppermute(block, axis, route)


def line_gather(piece):
    n = lax.axis_size("seq")
    here = lax.axis_index("seq")
    from_right = [piece]
    from_left = [piece]
    for k in range(1, n):
        from_right.append(lax.ppermute(from_right[-1], "seq", [(j, j - 1) for j in range(1, n - k + 1)]))
        from_left.append(lax.ppermute(from_left[-1], "seq", [(j, j + 1) for j in range(k - 1, n - 1)]))
    slots = [piece]
    for m in range(1, n):
        slots.append(jnp.where(here + m < n, from_right[m], from_left[n - m]))
    return jnp.concatenate(slots, axis=0)


def swap_gather(piece, axis, dim):
    if lax.axis_size(axis) != 2:
        return lax.all_gather(piece, axis, axis=dim, tiled=True)
    first = lax.axis_index(axis) == 0
    other = lax.ppermute(piece, axis, [(0, 1), (1, 0)])
    low = jnp.where(first, piece, other)
    high = jnp.where(first, other, piece)
    return jnp.concatenate([low, high], axis=dim)


def full_columns(weight, shared, after=None):
    if not shared:
        return [lax.all_gather(weight, "seq", axis=0, tiled=True)]
    rows, half = weight.shape[0], weight.shape[1] // 2
    group = lax.axis_index("groups")
    own = lax.dynamic_slice_in_dim(weight, group * half, half, axis=1)
    kept = lax.dynamic_slice_in_dim(weight, (1 - group) * half, half, axis=1)
    own = lax.all_gather(own, "seq", axis=0, tiled=True)
    if after is not None:
        own = lax.optimization_barrier((own, after))[0]
    own = jnp.roll(own, -lax.axis_index("seq") * rows, axis=0)
    split = rows + (own.shape[0] - rows) // 2
    first = lax.ppermute(own[rows:split], "groups", [(0, 1), (1, 0)])
    second = lax.ppermute(own[split:], "groups", [(0, 1), (1, 0)])
    return [own, jnp.concatenate([kept, first, second], axis=0)]


def per_device(acts, w_query, w_key, w_value):
    block = swap_gather(acts, "row", 0)
    block = swap_gather(block, "col", 1)
    tokens_here = block.shape[0]
    width = w_query.shape[1]
    heads_here = width // HD
    shared = lax.axis_size("groups") == 2 and width % (2 * HD) == 0
    if shared:
        block = jnp.roll(block, -lax.axis_index("seq") * w_query.shape[0], axis=1)

    def project(weight, after=None):
        return [
            jnp.dot(block, piece, preferred_element_type=jnp.float32).astype(jnp.bfloat16)
            for piece in full_columns(weight, shared, after)
        ]

    key = jnp.concatenate(project(w_key), axis=1)
    value = jnp.concatenate(project(w_value), axis=1)
    queries = project(w_query, key)
    if lax.axis_size("seq") == SPAN:
        seen = jnp.stack([line_gather(key), line_gather(value)])
    else:
        packed = jnp.stack([key, value])
        blocks_seen = [packed]
        current = packed
        for step in range(1, SPAN):
            current = passed_along(current, "seq", 1)
            blocks_seen.append(current)
        seen = jnp.concatenate(blocks_seen, axis=1)
    seen_keys = seen[0].reshape(-1, heads_here, HD)
    seen_values = seen[1].reshape(-1, heads_here, HD)
    scale = 1.0 / jnp.sqrt(jnp.float32(HD))
    outputs = []
    first = 0
    for query in queries:
        count = query.shape[1] // HD
        query = query.reshape(tokens_here, count, HD)
        part_keys = seen_keys[:, first : first + count]
        part_values = seen_values[:, first : first + count]
        first += count
        scores = jnp.einsum("qhd,khd->hqk", query, part_keys, preferred_element_type=jnp.float32) * scale
        largest = scores.max(axis=-1, keepdims=True)
        expos = jnp.exp(scores - largest)
        running_total = jnp.sum(expos, axis=-1)
        summed = jnp.einsum(
            "hqk,khd->qhd", expos.astype(jnp.bfloat16), part_values, preferred_element_type=jnp.float32
        )
        attended = summed / jnp.transpose(running_total)[:, :, None]
        outputs.append(attended.astype(jnp.bfloat16).reshape(tokens_here, count * HD))
    attended = jnp.concatenate(outputs, axis=1)
    if shared:
        attended = jnp.roll(attended, lax.axis_index("groups") * (width // 2), axis=1)
    return attended


def solution(mesh):
    in_specs = (
        P(("groups", "seq", "row"), "col"),
        P("seq", ("row", "col")),
        P("seq", ("row", "col")),
        P("seq", ("row", "col")),
    )
    out_specs = P(("groups", "seq"), ("row", "col"))
    return jax.shard_map(
        per_device, mesh=mesh, in_specs=in_specs, out_specs=out_specs, check_vma=False
    )
```

```python
import jax
import jax.numpy as jnp
from jax import lax
from jax.sharding import PartitionSpec as P

HD = 128
SPAN = 4


def passed_along(block, axis, distance):
    devices = range(lax.axis_size(axis))
    route = [((i - distance) % len(devices), i) for i in devices]
    return lax.ppermute(block, axis, route)


def line_gather(piece):
    n = lax.axis_size("seq")
    here = lax.axis_index("seq")
    from_right = [piece]
    from_left = [piece]
    for k in range(1, n):
        from_right.append(lax.ppermute(from_right[-1], "seq", [(j, j - 1) for j in range(1, n - k + 1)]))
        from_left.append(lax.ppermute(from_left[-1], "seq", [(j, j + 1) for j in range(k - 1, n - 1)]))
    slots = [piece]
    for m in range(1, n):
        slots.append(jnp.where(here + m < n, from_right[m], from_left[n - m]))
    return jnp.concatenate(slots, axis=0)


def swap_gather(piece, axis, dim):
    if lax.axis_size(axis) != 2:
        return lax.all_gather(piece, axis, axis=dim, tiled=True)
    first = lax.axis_index(axis) == 0
    other = lax.ppermute(piece, axis, [(0, 1), (1, 0)])
    low = jnp.where(first, piece, other)
    high = jnp.where(first, other, piece)
    return jnp.concatenate([low, high], axis=dim)


def full_columns(weight, shared, after=None):
    if not shared:
        return [lax.all_gather(weight, "seq", axis=0, tiled=True)]
    rows, half = weight.shape[0], weight.shape[1] // 2
    group = lax.axis_index("groups")
    own = lax.dynamic_slice_in_dim(weight, group * half, half, axis=1)
    kept = lax.dynamic_slice_in_dim(weight, (1 - group) * half, half, axis=1)
    own = lax.all_gather(own, "seq", axis=0, tiled=True)
    own = jnp.roll(own, -lax.axis_index("seq") * rows, axis=0)
    if after is not None:
        own = lax.optimization_barrier((own, after))[0]
    other = lax.ppermute(own[rows:], "groups", [(0, 1), (1, 0)])
    return [own, jnp.concatenate([kept, other], axis=0)]


def chained_columns(weight):
    n = lax.axis_size("seq")
    here = lax.axis_index("seq")
    half = weight.shape[1] // 2
    group = lax.axis_index("groups")
    own = lax.dynamic_slice_in_dim(weight, group * half, half, axis=1)
    kept = lax.dynamic_slice_in_dim(weight, (1 - group) * half, half, axis=1)

    def across(piece, places):
        pairs = [(g * n + j, (1 - g) * n + j) for g in range(2) for j in places]
        return lax.ppermute(piece, ("groups", "seq"), pairs)

    right, left = [own], [own]
    right_other, left_other = [kept], [kept]
    for k in range(1, n):
        right.append(lax.ppermute(right[-1], "seq", [(j, j - 1) for j in range(1, n - k + 1)]))
        left.append(lax.ppermute(left[-1], "seq", [(j, j + 1) for j in range(k - 1, n - 1)]))
        right_other.append(across(right[k], range(0, n - k)))
        left_other.append(across(left[k], range(k, n)))

    def slots(first, from_right, from_left):
        chosen = [first]
        for m in range(1, n):
            chosen.append(jnp.where(here + m < n, from_right[m], from_left[n - m]))
        return jnp.concatenate(chosen, axis=0)

    return [slots(own, right, left), slots(kept, right_other, left_other)]


def per_device(acts, w_query, w_key, w_value):
    block = swap_gather(acts, "row", 0)
    block = swap_gather(block, "col", 1)
    tokens_here = block.shape[0]
    width = w_query.shape[1]
    heads_here = width // HD
    shared = lax.axis_size("groups") == 2 and width % (2 * HD) == 0
    if shared:
        block = jnp.roll(block, -lax.axis_index("seq") * w_query.shape[0], axis=1)

    def project(weight, after=None):
        return [
            jnp.dot(block, piece, preferred_element_type=jnp.float32).astype(jnp.bfloat16)
            for piece in full_columns(weight, shared, after)
        ]

    if shared and lax.axis_size("seq") == SPAN:
        key = jnp.concatenate(
            [
                jnp.dot(block, piece, preferred_element_type=jnp.float32).astype(jnp.bfloat16)
                for piece in chained_columns(w_key)
            ],
            axis=1,
        )
    else:
        key = jnp.concatenate(project(w_key), axis=1)
    value = jnp.concatenate(project(w_value), axis=1)
    queries = project(w_query, key)
    if lax.axis_size("seq") == SPAN:
        seen = jnp.stack([line_gather(key), line_gather(value)])
    else:
        packed = jnp.stack([key, value])
        blocks_seen = [packed]
        current = packed
        for step in range(1, SPAN):
            current = passed_along(current, "seq", 1)
            blocks_seen.append(current)
        seen = jnp.concatenate(blocks_seen, axis=1)
    seen_keys = seen[0].reshape(-1, heads_here, HD)
    seen_values = seen[1].reshape(-1, heads_here, HD)
    scale = 1.0 / jnp.sqrt(jnp.float32(HD))
    outputs = []
    first = 0
    for query in queries:
        count = query.shape[1] // HD
        query = query.reshape(tokens_here, count, HD)
        part_keys = seen_keys[:, first : first + count]
        part_values = seen_values[:, first : first + count]
        first += count
        scores = jnp.einsum("qhd,khd->hqk", query, part_keys, preferred_element_type=jnp.float32) * scale
        largest = scores.max(axis=-1, keepdims=True)
        expos = jnp.exp(scores - largest)
        running_total = jnp.sum(expos, axis=-1)
        summed = jnp.einsum(
            "hqk,khd->qhd", expos.astype(jnp.bfloat16), part_values, preferred_element_type=jnp.float32
        )
        attended = summed / jnp.transpose(running_total)[:, :, None]
        outputs.append(attended.astype(jnp.bfloat16).reshape(tokens_here, count * HD))
    attended = jnp.concatenate(outputs, axis=1)
    if shared:
        attended = jnp.roll(attended, lax.axis_index("groups") * (width // 2), axis=1)
    return attended


def solution(mesh):
    in_specs = (
        P(("groups", "seq", "row"), "col"),
        P("seq", ("row", "col")),
        P("seq", ("row", "col")),
        P("seq", ("row", "col")),
    )
    out_specs = P(("groups", "seq"), ("row", "col"))
    return jax.shard_map(
        per_device, mesh=mesh, in_specs=in_specs, out_specs=out_specs, check_vma=False
    )
```

```python
import jax
import jax.numpy as jnp
from jax import lax
from jax.sharding import PartitionSpec as P
from jax.experimental import pallas as pl

HD = 128
SPAN = 4


def passed_along(block, axis, distance):
    devices = range(lax.axis_size(axis))
    route = [((i - distance) % len(devices), i) for i in devices]
    return lax.ppermute(block, axis, route)


def line_gather(piece):
    n = lax.axis_size("seq")
    here = lax.axis_index("seq")
    from_right = [piece]
    from_left = [piece]
    for k in range(1, n):
        from_right.append(lax.ppermute(from_right[-1], "seq", [(j, j - 1) for j in range(1, n - k + 1)]))
        from_left.append(lax.ppermute(from_left[-1], "seq", [(j, j + 1) for j in range(k - 1, n - 1)]))
    slots = [piece]
    for m in range(1, n):
        slots.append(jnp.where(here + m < n, from_right[m], from_left[n - m]))
    return jnp.concatenate(slots, axis=0)


def swap_gather(piece, axis, dim):
    if lax.axis_size(axis) != 2:
        return lax.all_gather(piece, axis, axis=dim, tiled=True)
    first = lax.axis_index(axis) == 0
    other = lax.ppermute(piece, axis, [(0, 1), (1, 0)])
    low = jnp.where(first, piece, other)
    high = jnp.where(first, other, piece)
    return jnp.concatenate([low, high], axis=dim)


def full_columns(weight, shared, after=None):
    if not shared:
        return [lax.all_gather(weight, "seq", axis=0, tiled=True)]
    rows, half = weight.shape[0], weight.shape[1] // 2
    group = lax.axis_index("groups")
    own = lax.dynamic_slice_in_dim(weight, group * half, half, axis=1)
    kept = lax.dynamic_slice_in_dim(weight, (1 - group) * half, half, axis=1)
    own = lax.all_gather(own, "seq", axis=0, tiled=True)
    own = jnp.roll(own, -lax.axis_index("seq") * rows, axis=0)
    if after is not None:
        own = lax.optimization_barrier((own, after))[0]
    other = lax.ppermute(own[rows:], "groups", [(0, 1), (1, 0)])
    return [own, (kept, other)]


def late_kernel(block_ref, kept_ref, other_ref, keys_ref, values_ref, out_ref):
    rows = kept_ref.shape[0]
    query = jnp.dot(block_ref[:, :rows], kept_ref[...], preferred_element_type=jnp.float32)
    query = query + jnp.dot(block_ref[:, rows:], other_ref[...], preferred_element_type=jnp.float32)
    query = query.astype(jnp.bfloat16)
    scale = 1.0 / jnp.sqrt(jnp.float32(HD))
    for head in range(out_ref.shape[1] // HD):
        cols = slice(head * HD, (head + 1) * HD)
        scores = lax.dot_general(
            query[:, cols],
            keys_ref[:, cols],
            (((1,), (1,)), ((), ())),
            preferred_element_type=jnp.float32,
        ) * scale
        largest = scores.max(axis=-1, keepdims=True)
        expos = jnp.exp(scores - largest)
        total = expos.sum(axis=-1, keepdims=True)
        summed = jnp.dot(expos.astype(jnp.bfloat16), values_ref[:, cols], preferred_element_type=jnp.float32)
        out_ref[:, cols] = (summed / total).astype(jnp.bfloat16)


def late_half(block, kept, other, keys, values, interpret=False):
    return pl.pallas_call(
        late_kernel,
        out_shape=jax.ShapeDtypeStruct((block.shape[0], kept.shape[1]), jnp.bfloat16),
        interpret=interpret,
    )(block, kept, other, keys, values)


def per_device(acts, w_query, w_key, w_value):
    block = swap_gather(acts, "row", 0)
    block = swap_gather(block, "col", 1)
    tokens_here = block.shape[0]
    width = w_query.shape[1]
    heads_here = width // HD
    shared = lax.axis_size("groups") == 2 and width % (2 * HD) == 0
    if shared:
        block = jnp.roll(block, -lax.axis_index("seq") * w_query.shape[0], axis=1)

    def product(piece):
        if isinstance(piece, tuple):
            piece = jnp.concatenate(piece, axis=0)
        return jnp.dot(block, piece, preferred_element_type=jnp.float32).astype(jnp.bfloat16)

    key = jnp.concatenate([product(piece) for piece in full_columns(w_key, shared)], axis=1)
    value = jnp.concatenate([product(piece) for piece in full_columns(w_value, shared)], axis=1)
    queries = full_columns(w_query, shared, key)
    if lax.axis_size("seq") == SPAN:
        seen = jnp.stack([line_gather(key), line_gather(value)])
    else:
        packed = jnp.stack([key, value])
        blocks_seen = [packed]
        current = packed
        for step in range(1, SPAN):
            current = passed_along(current, "seq", 1)
            blocks_seen.append(current)
        seen = jnp.concatenate(blocks_seen, axis=1)
    seen_keys = seen[0].reshape(-1, heads_here, HD)
    seen_values = seen[1].reshape(-1, heads_here, HD)
    scale = 1.0 / jnp.sqrt(jnp.float32(HD))
    outputs = []
    first = 0
    for piece in queries:
        if isinstance(piece, tuple):
            count = piece[0].shape[1] // HD
            columns = slice(first * HD, (first + count) * HD)
            first += count
            outputs.append(late_half(block, piece[0], piece[1], seen[0][:, columns], seen[1][:, columns]))
            continue
        query = product(piece)
        count = query.shape[1] // HD
        query = query.reshape(tokens_here, count, HD)
        part_keys = seen_keys[:, first : first + count]
        part_values = seen_values[:, first : first + count]
        first += count
        scores = jnp.einsum("qhd,khd->hqk", query, part_keys, preferred_element_type=jnp.float32) * scale
        largest = scores.max(axis=-1, keepdims=True)
        expos = jnp.exp(scores - largest)
        running_total = jnp.sum(expos, axis=-1)
        summed = jnp.einsum(
            "hqk,khd->qhd", expos.astype(jnp.bfloat16), part_values, preferred_element_type=jnp.float32
        )
        attended = summed / jnp.transpose(running_total)[:, :, None]
        outputs.append(attended.astype(jnp.bfloat16).reshape(tokens_here, count * HD))
    attended = jnp.concatenate(outputs, axis=1)
    if shared:
        attended = jnp.roll(attended, lax.axis_index("groups") * (width // 2), axis=1)
    return attended


def solution(mesh):
    in_specs = (
        P(("groups", "seq", "row"), "col"),
        P("seq", ("row", "col")),
        P("seq", ("row", "col")),
        P("seq", ("row", "col")),
    )
    out_specs = P(("groups", "seq"), ("row", "col"))
    return jax.shard_map(
        per_device, mesh=mesh, in_specs=in_specs, out_specs=out_specs, check_vma=False
    )
```

```python
import jax
import jax.numpy as jnp
from jax import lax
from jax.sharding import PartitionSpec as P
from jax.experimental import pallas as pl

HD = 128
SPAN = 4


def passed_along(block, axis, distance):
    devices = range(lax.axis_size(axis))
    route = [((i - distance) % len(devices), i) for i in devices]
    return lax.ppermute(block, axis, route)


def line_gather(piece):
    n = lax.axis_size("seq")
    here = lax.axis_index("seq")
    from_right = [piece]
    from_left = [piece]
    for k in range(1, n):
        from_right.append(lax.ppermute(from_right[-1], "seq", [(j, j - 1) for j in range(1, n - k + 1)]))
        from_left.append(lax.ppermute(from_left[-1], "seq", [(j, j + 1) for j in range(k - 1, n - 1)]))
    slots = [piece]
    for m in range(1, n):
        slots.append(jnp.where(here + m < n, from_right[m], from_left[n - m]))
    return jnp.concatenate(slots, axis=0)


def swap_gather(piece, axis, dim):
    if lax.axis_size(axis) != 2:
        return lax.all_gather(piece, axis, axis=dim, tiled=True)
    first = lax.axis_index(axis) == 0
    other = lax.ppermute(piece, axis, [(0, 1), (1, 0)])
    low = jnp.where(first, piece, other)
    high = jnp.where(first, other, piece)
    return jnp.concatenate([low, high], axis=dim)


def full_columns(weight, shared, after=None):
    if not shared:
        return [lax.all_gather(weight, "seq", axis=0, tiled=True)]
    rows, half = weight.shape[0], weight.shape[1] // 2
    group = lax.axis_index("groups")
    own = lax.dynamic_slice_in_dim(weight, group * half, half, axis=1)
    kept = lax.dynamic_slice_in_dim(weight, (1 - group) * half, half, axis=1)
    own = lax.all_gather(own, "seq", axis=0, tiled=True)
    own = jnp.roll(own, -lax.axis_index("seq") * rows, axis=0)
    if after is not None:
        own = lax.optimization_barrier((own, after))[0]
    other = lax.ppermute(own[rows:], "groups", [(0, 1), (1, 0)])
    return [own, (kept, other)]


def late_kernel(early_ref, block_ref, other_ref, keys_ref, values_ref, out_ref):
    query = early_ref[...] + jnp.dot(block_ref[...], other_ref[...], preferred_element_type=jnp.float32)
    query = query.astype(jnp.bfloat16)
    scale = 1.0 / jnp.sqrt(jnp.float32(HD))
    for head in range(out_ref.shape[1] // HD):
        cols = slice(head * HD, (head + 1) * HD)
        scores = jnp.dot(query[:, cols], keys_ref[cols, :], preferred_element_type=jnp.float32) * scale
        largest = scores.max(axis=-1, keepdims=True)
        expos = jnp.exp(scores - largest)
        total = expos.sum(axis=-1, keepdims=True)
        summed = jnp.dot(expos.astype(jnp.bfloat16), values_ref[:, cols], preferred_element_type=jnp.float32)
        out_ref[:, cols] = (summed / total).astype(jnp.bfloat16)


def late_half(early, block, other, keys_t, values, interpret=False):
    return pl.pallas_call(
        late_kernel,
        out_shape=jax.ShapeDtypeStruct(early.shape, jnp.bfloat16),
        interpret=interpret,
    )(early, block, other, keys_t, values)


def per_device(acts, w_query, w_key, w_value):
    block = swap_gather(acts, "row", 0)
    block = swap_gather(block, "col", 1)
    tokens_here = block.shape[0]
    width = w_query.shape[1]
    heads_here = width // HD
    shared = lax.axis_size("groups") == 2 and width % (2 * HD) == 0
    if shared:
        block = jnp.roll(block, -lax.axis_index("seq") * w_query.shape[0], axis=1)

    def product(piece):
        if isinstance(piece, tuple):
            piece = jnp.concatenate(piece, axis=0)
        return jnp.dot(block, piece, preferred_element_type=jnp.float32).astype(jnp.bfloat16)

    key = jnp.concatenate([product(piece) for piece in full_columns(w_key, shared)], axis=1)
    value = jnp.concatenate([product(piece) for piece in full_columns(w_value, shared)], axis=1)
    queries = full_columns(w_query, shared, key)
    if lax.axis_size("seq") == SPAN:
        seen = jnp.stack([line_gather(key), line_gather(value)])
    else:
        packed = jnp.stack([key, value])
        blocks_seen = [packed]
        current = packed
        for step in range(1, SPAN):
            current = passed_along(current, "seq", 1)
            blocks_seen.append(current)
        seen = jnp.concatenate(blocks_seen, axis=1)
    seen_keys = seen[0].reshape(-1, heads_here, HD)
    seen_values = seen[1].reshape(-1, heads_here, HD)
    scale = 1.0 / jnp.sqrt(jnp.float32(HD))
    outputs = []
    first = 0
    for piece in queries:
        if isinstance(piece, tuple):
            count = piece[0].shape[1] // HD
            columns = slice(first * HD, (first + count) * HD)
            first += count
            rows = piece[0].shape[0]
            early = jnp.dot(block[:, :rows], piece[0], preferred_element_type=jnp.float32)
            outputs.append(
                late_half(early, block[:, rows:], piece[1], seen[0][:, columns].T, seen[1][:, columns])
            )
            continue
        query = product(piece)
        count = query.shape[1] // HD
        query = query.reshape(tokens_here, count, HD)
        part_keys = seen_keys[:, first : first + count]
        part_values = seen_values[:, first : first + count]
        first += count
        scores = jnp.einsum("qhd,khd->hqk", query, part_keys, preferred_element_type=jnp.float32) * scale
        largest = scores.max(axis=-1, keepdims=True)
        expos = jnp.exp(scores - largest)
        running_total = jnp.sum(expos, axis=-1)
        summed = jnp.einsum(
            "hqk,khd->qhd", expos.astype(jnp.bfloat16), part_values, preferred_element_type=jnp.float32
        )
        attended = summed / jnp.transpose(running_total)[:, :, None]
        outputs.append(attended.astype(jnp.bfloat16).reshape(tokens_here, count * HD))
    attended = jnp.concatenate(outputs, axis=1)
    if shared:
        attended = jnp.roll(attended, lax.axis_index("groups") * (width // 2), axis=1)
    return attended


def solution(mesh):
    in_specs = (
        P(("groups", "seq", "row"), "col"),
        P("seq", ("row", "col")),
        P("seq", ("row", "col")),
        P("seq", ("row", "col")),
    )
    out_specs = P(("groups", "seq"), ("row", "col"))
    return jax.shard_map(
        per_device, mesh=mesh, in_specs=in_specs, out_specs=out_specs, check_vma=False
    )
```

```python
import jax
import jax.numpy as jnp
from jax import lax
from jax.sharding import PartitionSpec as P

HD = 128
SPAN = 4


def passed_along(block, axis, distance):
    devices = range(lax.axis_size(axis))
    route = [((i - distance) % len(devices), i) for i in devices]
    return lax.ppermute(block, axis, route)


def line_gather(piece):
    n = lax.axis_size("seq")
    here = lax.axis_index("seq")
    from_right = [piece]
    from_left = [piece]
    for k in range(1, n):
        from_right.append(lax.ppermute(from_right[-1], "seq", [(j, j - 1) for j in range(1, n - k + 1)]))
        from_left.append(lax.ppermute(from_left[-1], "seq", [(j, j + 1) for j in range(k - 1, n - 1)]))
    slots = [piece]
    for m in range(1, n):
        slots.append(jnp.where(here + m < n, from_right[m], from_left[n - m]))
    return jnp.concatenate(slots, axis=0)


def swap_gather(piece, axis, dim):
    if lax.axis_size(axis) != 2:
        return lax.all_gather(piece, axis, axis=dim, tiled=True)
    first = lax.axis_index(axis) == 0
    other = lax.ppermute(piece, axis, [(0, 1), (1, 0)])
    low = jnp.where(first, piece, other)
    high = jnp.where(first, other, piece)
    return jnp.concatenate([low, high], axis=dim)


def full_columns(weight, shared, after=None):
    if not shared:
        return [lax.all_gather(weight, "seq", axis=0, tiled=True)]
    rows, half = weight.shape[0], weight.shape[1] // 2
    group = lax.axis_index("groups")
    own = lax.dynamic_slice_in_dim(weight, group * half, half, axis=1)
    kept = lax.dynamic_slice_in_dim(weight, (1 - group) * half, half, axis=1)
    own = lax.all_gather(own, "seq", axis=0, tiled=True)
    own = jnp.roll(own, -lax.axis_index("seq") * rows, axis=0)
    if after is not None:
        own, after = lax.optimization_barrier((own, after))
        other = lax.ppermute(own[rows:], "groups", [(0, 1), (1, 0)])
        return [own, jnp.concatenate([kept, other], axis=0)], after
    other = lax.ppermute(own[rows:], "groups", [(0, 1), (1, 0)])
    return [own, jnp.concatenate([kept, other], axis=0)]


def per_device(acts, w_query, w_key, w_value):
    block = swap_gather(acts, "row", 0)
    block = swap_gather(block, "col", 1)
    tokens_here = block.shape[0]
    width = w_query.shape[1]
    heads_here = width // HD
    shared = lax.axis_size("groups") == 2 and width % (2 * HD) == 0
    if shared:
        block = jnp.roll(block, -lax.axis_index("seq") * w_query.shape[0], axis=1)

    def project(pieces):
        return [
            jnp.dot(block, piece, preferred_element_type=jnp.float32).astype(jnp.bfloat16)
            for piece in pieces
        ]

    key = jnp.concatenate(project(full_columns(w_key, shared)), axis=1)
    value = jnp.concatenate(project(full_columns(w_value, shared)), axis=1)
    if shared:
        query_pieces, key = full_columns(w_query, shared, key)
    else:
        query_pieces = full_columns(w_query, shared)
    queries = project(query_pieces)
    if lax.axis_size("seq") == SPAN:
        seen = jnp.stack([line_gather(key), line_gather(value)])
    else:
        packed = jnp.stack([key, value])
        blocks_seen = [packed]
        current = packed
        for step in range(1, SPAN):
            current = passed_along(current, "seq", 1)
            blocks_seen.append(current)
        seen = jnp.concatenate(blocks_seen, axis=1)
    seen_keys = seen[0].reshape(-1, heads_here, HD)
    seen_values = seen[1].reshape(-1, heads_here, HD)
    scale = 1.0 / jnp.sqrt(jnp.float32(HD))
    outputs = []
    first = 0
    for query in queries:
        count = query.shape[1] // HD
        query = query.reshape(tokens_here, count, HD)
        part_keys = seen_keys[:, first : first + count]
        part_values = seen_values[:, first : first + count]
        first += count
        scores = jnp.einsum("qhd,khd->hqk", query, part_keys, preferred_element_type=jnp.float32) * scale
        largest = scores.max(axis=-1, keepdims=True)
        expos = jnp.exp(scores - largest)
        running_total = jnp.sum(expos, axis=-1)
        summed = jnp.einsum(
            "hqk,khd->qhd", expos.astype(jnp.bfloat16), part_values, preferred_element_type=jnp.float32
        )
        attended = summed / jnp.transpose(running_total)[:, :, None]
        outputs.append(attended.astype(jnp.bfloat16).reshape(tokens_here, count * HD))
    attended = jnp.concatenate(outputs, axis=1)
    if shared:
        attended = jnp.roll(attended, lax.axis_index("groups") * (width // 2), axis=1)
    return attended


def solution(mesh):
    in_specs = (
        P(("groups", "seq", "row"), "col"),
        P("seq", ("row", "col")),
        P("seq", ("row", "col")),
        P("seq", ("row", "col")),
    )
    out_specs = P(("groups", "seq"), ("row", "col"))
    return jax.shard_map(
        per_device, mesh=mesh, in_specs=in_specs, out_specs=out_specs, check_vma=False
    )
```

```python
import jax
import jax.numpy as jnp
from jax import lax
from jax.sharding import PartitionSpec as P

HD = 128
SPAN = 4


def passed_along(block, axis, distance):
    devices = range(lax.axis_size(axis))
    route = [((i - distance) % len(devices), i) for i in devices]
    return lax.ppermute(block, axis, route)


def line_gather(piece):
    n = lax.axis_size("seq")
    here = lax.axis_index("seq")
    from_right = [piece]
    from_left = [piece]
    for k in range(1, n):
        from_right.append(lax.ppermute(from_right[-1], "seq", [(j, j - 1) for j in range(1, n - k + 1)]))
        from_left.append(lax.ppermute(from_left[-1], "seq", [(j, j + 1) for j in range(k - 1, n - 1)]))
    slots = [piece]
    for m in range(1, n):
        slots.append(jnp.where(here + m < n, from_right[m], from_left[n - m]))
    return jnp.concatenate(slots, axis=0)


def swap_gather(piece, axis, dim):
    if lax.axis_size(axis) != 2:
        return lax.all_gather(piece, axis, axis=dim, tiled=True)
    first = lax.axis_index(axis) == 0
    other = lax.ppermute(piece, axis, [(0, 1), (1, 0)])
    low = jnp.where(first, piece, other)
    high = jnp.where(first, other, piece)
    return jnp.concatenate([low, high], axis=dim)


def full_columns(weight, shared, after=None):
    if not shared:
        return [lax.all_gather(weight, "seq", axis=0, tiled=True)]
    rows, half = weight.shape[0], weight.shape[1] // 2
    group = lax.axis_index("groups")
    own = lax.dynamic_slice_in_dim(weight, group * half, half, axis=1)
    kept = lax.dynamic_slice_in_dim(weight, (1 - group) * half, half, axis=1)
    own = lax.all_gather(own, "seq", axis=0, tiled=True)
    own = jnp.roll(own, -lax.axis_index("seq") * rows, axis=0)
    if after is not None:
        own = lax.optimization_barrier((own, after))[0]
    other = lax.ppermute(own[rows:], "groups", [(0, 1), (1, 0)])
    return [own, jnp.concatenate([kept, other], axis=0)]


def query_columns(weight, after):
    n = lax.axis_size("seq")
    rows, half = weight.shape[0], weight.shape[1] // 2
    group = lax.axis_index("groups")
    own = lax.dynamic_slice_in_dim(weight, group * half, half, axis=1)
    kept = lax.dynamic_slice_in_dim(weight, (1 - group) * half, half, axis=1)
    gathered = lax.all_gather(own, "seq", axis=0, tiled=True)
    gathered = lax.optimization_barrier((gathered, after))[0]
    received = []
    for j in range(n):
        pairs = [(g * n + i, (1 - g) * n + i) for g in range(2) for i in range(n) if i != j]
        received.append(lax.ppermute(gathered[j * rows : (j + 1) * rows], ("groups", "seq"), pairs))
    return gathered, kept, jnp.concatenate(received, axis=0)


def per_device(acts, w_query, w_key, w_value):
    block = swap_gather(acts, "row", 0)
    block = swap_gather(block, "col", 1)
    unrolled = block
    tokens_here = block.shape[0]
    width = w_query.shape[1]
    heads_here = width // HD
    shared = lax.axis_size("groups") == 2 and width % (2 * HD) == 0
    if shared:
        block = jnp.roll(block, -lax.axis_index("seq") * w_query.shape[0], axis=1)

    def project(weight, after=None):
        return [
            jnp.dot(block, piece, preferred_element_type=jnp.float32).astype(jnp.bfloat16)
            for piece in full_columns(weight, shared, after)
        ]

    key = jnp.concatenate(project(w_key), axis=1)
    value = jnp.concatenate(project(w_value), axis=1)
    if shared and lax.axis_size("seq") == SPAN:
        gathered, kept, received = query_columns(w_query, key)
        rows = kept.shape[0]
        held = lax.dynamic_slice_in_dim(unrolled, lax.axis_index("seq") * rows, rows, axis=1)
        early = jnp.dot(held, kept, preferred_element_type=jnp.float32)
        late = jnp.dot(unrolled, received, preferred_element_type=jnp.float32)
        queries = [
            jnp.dot(unrolled, gathered, preferred_element_type=jnp.float32).astype(jnp.bfloat16),
            (early + late).astype(jnp.bfloat16),
        ]
    else:
        queries = project(w_query, key)
    if lax.axis_size("seq") == SPAN:
        seen = jnp.stack([line_gather(key), line_gather(value)])
    else:
        packed = jnp.stack([key, value])
        blocks_seen = [packed]
        current = packed
        for step in range(1, SPAN):
            current = passed_along(current, "seq", 1)
            blocks_seen.append(current)
        seen = jnp.concatenate(blocks_seen, axis=1)
    seen_keys = seen[0].reshape(-1, heads_here, HD)
    seen_values = seen[1].reshape(-1, heads_here, HD)
    scale = 1.0 / jnp.sqrt(jnp.float32(HD))
    outputs = []
    first = 0
    for query in queries:
        count = query.shape[1] // HD
        query = query.reshape(tokens_here, count, HD)
        part_keys = seen_keys[:, first : first + count]
        part_values = seen_values[:, first : first + count]
        first += count
        scores = jnp.einsum("qhd,khd->hqk", query, part_keys, preferred_element_type=jnp.float32) * scale
        largest = scores.max(axis=-1, keepdims=True)
        expos = jnp.exp(scores - largest)
        running_total = jnp.sum(expos, axis=-1)
        summed = jnp.einsum(
            "hqk,khd->qhd", expos.astype(jnp.bfloat16), part_values, preferred_element_type=jnp.float32
        )
        attended = summed / jnp.transpose(running_total)[:, :, None]
        outputs.append(attended.astype(jnp.bfloat16).reshape(tokens_here, count * HD))
    attended = jnp.concatenate(outputs, axis=1)
    if shared:
        attended = jnp.roll(attended, lax.axis_index("groups") * (width // 2), axis=1)
    return attended


def solution(mesh):
    in_specs = (
        P(("groups", "seq", "row"), "col"),
        P("seq", ("row", "col")),
        P("seq", ("row", "col")),
        P("seq", ("row", "col")),
    )
    out_specs = P(("groups", "seq"), ("row", "col"))
    return jax.shard_map(
        per_device, mesh=mesh, in_specs=in_specs, out_specs=out_specs, check_vma=False
    )
```

```python
import jax
import jax.numpy as jnp
from jax import lax
from jax.sharding import PartitionSpec as P

HD = 128
SPAN = 4


def passed_along(block, axis, distance):
    devices = range(lax.axis_size(axis))
    route = [((i - distance) % len(devices), i) for i in devices]
    return lax.ppermute(block, axis, route)


def line_gather(piece, gate=None):
    n = lax.axis_size("seq")
    here = lax.axis_index("seq")
    from_right = [piece]
    from_left = [piece]
    for k in range(1, n):
        if k == 2 and gate is not None:
            from_right[-1], from_left[-1], _ = lax.optimization_barrier((from_right[-1], from_left[-1], gate))
        from_right.append(lax.ppermute(from_right[-1], "seq", [(j, j - 1) for j in range(1, n - k + 1)]))
        from_left.append(lax.ppermute(from_left[-1], "seq", [(j, j + 1) for j in range(k - 1, n - 1)]))
    slots = [piece]
    for m in range(1, n):
        slots.append(jnp.where(here + m < n, from_right[m], from_left[n - m]))
    return jnp.concatenate(slots, axis=0)


def swap_gather(piece, axis, dim):
    if lax.axis_size(axis) != 2:
        return lax.all_gather(piece, axis, axis=dim, tiled=True)
    first = lax.axis_index(axis) == 0
    other = lax.ppermute(piece, axis, [(0, 1), (1, 0)])
    low = jnp.where(first, piece, other)
    high = jnp.where(first, other, piece)
    return jnp.concatenate([low, high], axis=dim)


def full_columns(weight, shared, after=None):
    if not shared:
        return [lax.all_gather(weight, "seq", axis=0, tiled=True)]
    rows, half = weight.shape[0], weight.shape[1] // 2
    group = lax.axis_index("groups")
    own = lax.dynamic_slice_in_dim(weight, group * half, half, axis=1)
    kept = lax.dynamic_slice_in_dim(weight, (1 - group) * half, half, axis=1)
    own = lax.all_gather(own, "seq", axis=0, tiled=True)
    own = jnp.roll(own, -lax.axis_index("seq") * rows, axis=0)
    if after is not None:
        own = lax.optimization_barrier((own, after))[0]
    other = lax.ppermute(own[rows:], "groups", [(0, 1), (1, 0)])
    return [own, jnp.concatenate([kept, other], axis=0)]


def per_device(acts, w_query, w_key, w_value):
    block = swap_gather(acts, "row", 0)
    block = swap_gather(block, "col", 1)
    tokens_here = block.shape[0]
    width = w_query.shape[1]
    heads_here = width // HD
    shared = lax.axis_size("groups") == 2 and width % (2 * HD) == 0
    if shared:
        block = jnp.roll(block, -lax.axis_index("seq") * w_query.shape[0], axis=1)

    def project(weight, after=None):
        return [
            jnp.dot(block, piece, preferred_element_type=jnp.float32).astype(jnp.bfloat16)
            for piece in full_columns(weight, shared, after)
        ]

    key = jnp.concatenate(project(w_key), axis=1)
    value = jnp.concatenate(project(w_value), axis=1)
    query_pieces = full_columns(w_query, shared, key)
    queries = [
        jnp.dot(block, piece, preferred_element_type=jnp.float32).astype(jnp.bfloat16)
        for piece in query_pieces
    ]
    if lax.axis_size("seq") == SPAN:
        gate = query_pieces[0] if shared else None
        seen = jnp.stack([line_gather(key, gate), line_gather(value, gate)])
    else:
        packed = jnp.stack([key, value])
        blocks_seen = [packed]
        current = packed
        for step in range(1, SPAN):
            current = passed_along(current, "seq", 1)
            blocks_seen.append(current)
        seen = jnp.concatenate(blocks_seen, axis=1)
    seen_keys = seen[0].reshape(-1, heads_here, HD)
    seen_values = seen[1].reshape(-1, heads_here, HD)
    scale = 1.0 / jnp.sqrt(jnp.float32(HD))
    outputs = []
    first = 0
    for query in queries:
        count = query.shape[1] // HD
        query = query.reshape(tokens_here, count, HD)
        part_keys = seen_keys[:, first : first + count]
        part_values = seen_values[:, first : first + count]
        first += count
        scores = jnp.einsum("qhd,khd->hqk", query, part_keys, preferred_element_type=jnp.float32) * scale
        largest = scores.max(axis=-1, keepdims=True)
        expos = jnp.exp(scores - largest)
        running_total = jnp.sum(expos, axis=-1)
        summed = jnp.einsum(
            "hqk,khd->qhd", expos.astype(jnp.bfloat16), part_values, preferred_element_type=jnp.float32
        )
        attended = summed / jnp.transpose(running_total)[:, :, None]
        outputs.append(attended.astype(jnp.bfloat16).reshape(tokens_here, count * HD))
    attended = jnp.concatenate(outputs, axis=1)
    if shared:
        attended = jnp.roll(attended, lax.axis_index("groups") * (width // 2), axis=1)
    return attended


def solution(mesh):
    in_specs = (
        P(("groups", "seq", "row"), "col"),
        P("seq", ("row", "col")),
        P("seq", ("row", "col")),
        P("seq", ("row", "col")),
    )
    out_specs = P(("groups", "seq"), ("row", "col"))
    return jax.shard_map(
        per_device, mesh=mesh, in_specs=in_specs, out_specs=out_specs, check_vma=False
    )
```

```python
import jax
import jax.numpy as jnp
from jax import lax
from jax.sharding import PartitionSpec as P

HD = 128
SPAN = 4


def passed_along(block, axis, distance):
    devices = range(lax.axis_size(axis))
    route = [((i - distance) % len(devices), i) for i in devices]
    return lax.ppermute(block, axis, route)


def line_gather(piece):
    n = lax.axis_size("seq")
    here = lax.axis_index("seq")
    from_right = [piece]
    from_left = [piece]
    for k in range(1, n):
        from_right.append(lax.ppermute(from_right[-1], "seq", [(j, j - 1) for j in range(1, n - k + 1)]))
        from_left.append(lax.ppermute(from_left[-1], "seq", [(j, j + 1) for j in range(k - 1, n - 1)]))
    slots = [piece]
    for m in range(1, n):
        slots.append(jnp.where(here + m < n, from_right[m], from_left[n - m]))
    return jnp.concatenate(slots, axis=0)


def swap_gather(piece, axis, dim):
    if lax.axis_size(axis) != 2:
        return lax.all_gather(piece, axis, axis=dim, tiled=True)
    first = lax.axis_index(axis) == 0
    other = lax.ppermute(piece, axis, [(0, 1), (1, 0)])
    low = jnp.where(first, piece, other)
    high = jnp.where(first, other, piece)
    return jnp.concatenate([low, high], axis=dim)


def full_columns(weight, shared, after=None, gate=None):
    if not shared:
        return [lax.all_gather(weight, "seq", axis=0, tiled=True)]
    rows, half = weight.shape[0], weight.shape[1] // 2
    group = lax.axis_index("groups")
    count = 2 if gate is not None and half % (2 * HD) == 0 else 1
    width = half // count
    owns, others = [], []
    for k in range(count):
        own = lax.dynamic_slice_in_dim(weight, group * half + k * width, width, axis=1)
        kept = lax.dynamic_slice_in_dim(weight, (1 - group) * half + k * width, width, axis=1)
        if gate is not None:
            own, gate = lax.optimization_barrier((own, gate))
        own = lax.all_gather(own, "seq", axis=0, tiled=True)
        if others:
            own, others[-1] = lax.optimization_barrier((own, others[-1]))
        own = jnp.roll(own, -lax.axis_index("seq") * rows, axis=0)
        if after is not None:
            own, after = lax.optimization_barrier((own, after))
        other = lax.ppermute(own[rows:], "groups", [(0, 1), (1, 0)])
        owns.append(own)
        others.append(jnp.concatenate([kept, other], axis=0))
    return owns + others


def per_device(acts, w_query, w_key, w_value):
    block = swap_gather(acts, "row", 0)
    block = swap_gather(block, "col", 1)
    tokens_here = block.shape[0]
    width = w_query.shape[1]
    heads_here = width // HD
    shared = lax.axis_size("groups") == 2 and width % (2 * HD) == 0
    if shared:
        block = jnp.roll(block, -lax.axis_index("seq") * w_query.shape[0], axis=1)

    def project(pieces):
        return [
            jnp.dot(block, piece, preferred_element_type=jnp.float32).astype(jnp.bfloat16)
            for piece in pieces
        ]

    key = jnp.concatenate(project(full_columns(w_key, shared)), axis=1)
    value_pieces = full_columns(w_value, shared)
    value = jnp.concatenate(project(value_pieces), axis=1)
    gate = value_pieces[0] if shared else None
    queries = project(full_columns(w_query, shared, key, gate))
    if lax.axis_size("seq") == SPAN:
        seen = jnp.stack([line_gather(key), line_gather(value)])
    else:
        packed = jnp.stack([key, value])
        blocks_seen = [packed]
        current = packed
        for step in range(1, SPAN):
            current = passed_along(current, "seq", 1)
            blocks_seen.append(current)
        seen = jnp.concatenate(blocks_seen, axis=1)
    seen_keys = seen[0].reshape(-1, heads_here, HD)
    seen_values = seen[1].reshape(-1, heads_here, HD)
    scale = 1.0 / jnp.sqrt(jnp.float32(HD))
    outputs = []
    first = 0
    for query in queries:
        count = query.shape[1] // HD
        query = query.reshape(tokens_here, count, HD)
        part_keys = seen_keys[:, first : first + count]
        part_values = seen_values[:, first : first + count]
        first += count
        scores = jnp.einsum("qhd,khd->hqk", query, part_keys, preferred_element_type=jnp.float32) * scale
        largest = scores.max(axis=-1, keepdims=True)
        expos = jnp.exp(scores - largest)
        running_total = jnp.sum(expos, axis=-1)
        summed = jnp.einsum(
            "hqk,khd->qhd", expos.astype(jnp.bfloat16), part_values, preferred_element_type=jnp.float32
        )
        attended = summed / jnp.transpose(running_total)[:, :, None]
        outputs.append(attended.astype(jnp.bfloat16).reshape(tokens_here, count * HD))
    attended = jnp.concatenate(outputs, axis=1)
    if shared:
        attended = jnp.roll(attended, lax.axis_index("groups") * (width // 2), axis=1)
    return attended


def solution(mesh):
    in_specs = (
        P(("groups", "seq", "row"), "col"),
        P("seq", ("row", "col")),
        P("seq", ("row", "col")),
        P("seq", ("row", "col")),
    )
    out_specs = P(("groups", "seq"), ("row", "col"))
    return jax.shard_map(
        per_device, mesh=mesh, in_specs=in_specs, out_specs=out_specs, check_vma=False
    )
```

```python
import jax
import jax.numpy as jnp
from jax import lax
from jax.sharding import PartitionSpec as P

HD = 128
SPAN = 4


def passed_along(block, axis, distance):
    devices = range(lax.axis_size(axis))
    route = [((i - distance) % len(devices), i) for i in devices]
    return lax.ppermute(block, axis, route)


def line_gather(piece):
    n = lax.axis_size("seq")
    here = lax.axis_index("seq")
    from_right = [piece]
    from_left = [piece]
    for k in range(1, n):
        from_right.append(lax.ppermute(from_right[-1], "seq", [(j, j - 1) for j in range(1, n - k + 1)]))
        from_left.append(lax.ppermute(from_left[-1], "seq", [(j, j + 1) for j in range(k - 1, n - 1)]))
    slots = [piece]
    for m in range(1, n):
        slots.append(jnp.where(here + m < n, from_right[m], from_left[n - m]))
    return jnp.concatenate(slots, axis=0)


def swap_gather(piece, axis, dim):
    if lax.axis_size(axis) != 2:
        return lax.all_gather(piece, axis, axis=dim, tiled=True)
    first = lax.axis_index(axis) == 0
    other = lax.ppermute(piece, axis, [(0, 1), (1, 0)])
    low = jnp.where(first, piece, other)
    high = jnp.where(first, other, piece)
    return jnp.concatenate([low, high], axis=dim)


def full_columns(weight, shared, after=None):
    if not shared:
        return [lax.all_gather(weight, "seq", axis=0, tiled=True)]
    rows, half = weight.shape[0], weight.shape[1] // 2
    group = lax.axis_index("groups")
    own = lax.dynamic_slice_in_dim(weight, group * half, half, axis=1)
    kept = lax.dynamic_slice_in_dim(weight, (1 - group) * half, half, axis=1)
    own = lax.all_gather(own, "seq", axis=0, tiled=True)
    own = jnp.roll(own, -lax.axis_index("seq") * rows, axis=0)
    if after is not None:
        own = lax.optimization_barrier((own, after))[0]
    other = lax.ppermute(own[rows:], "groups", [(0, 1), (1, 0)])
    return [own, jnp.concatenate([kept, other], axis=0)]


def per_device(acts, w_query, w_key, w_value):
    block = swap_gather(acts, "row", 0)
    block = swap_gather(block, "col", 1)
    tokens_here = block.shape[0]
    width = w_query.shape[1]
    heads_here = width // HD
    shared = lax.axis_size("groups") == 2 and width % (2 * HD) == 0
    if shared:
        block = jnp.roll(block, -lax.axis_index("seq") * w_query.shape[0], axis=1)

    def project(weight, after=None):
        return [
            jnp.dot(block, piece, preferred_element_type=jnp.float32).astype(jnp.bfloat16)
            for piece in full_columns(weight, shared, after)
        ]

    key = jnp.concatenate(project(w_key), axis=1)
    value = jnp.concatenate(project(w_value), axis=1)
    queries = project(w_query, key)
    if lax.axis_size("seq") == SPAN:
        values_seen = lax.all_gather(value, "seq", axis=0, tiled=True)
        values_seen = jnp.roll(values_seen, -lax.axis_index("seq") * value.shape[0], axis=0)
        seen = jnp.stack([line_gather(key), values_seen])
    else:
        packed = jnp.stack([key, value])
        blocks_seen = [packed]
        current = packed
        for step in range(1, SPAN):
            current = passed_along(current, "seq", 1)
            blocks_seen.append(current)
        seen = jnp.concatenate(blocks_seen, axis=1)
    seen_keys = seen[0].reshape(-1, heads_here, HD)
    seen_values = seen[1].reshape(-1, heads_here, HD)
    scale = 1.0 / jnp.sqrt(jnp.float32(HD))
    outputs = []
    first = 0
    for query in queries:
        count = query.shape[1] // HD
        query = query.reshape(tokens_here, count, HD)
        part_keys = seen_keys[:, first : first + count]
        part_values = seen_values[:, first : first + count]
        first += count
        scores = jnp.einsum("qhd,khd->hqk", query, part_keys, preferred_element_type=jnp.float32) * scale
        largest = scores.max(axis=-1, keepdims=True)
        expos = jnp.exp(scores - largest)
        running_total = jnp.sum(expos, axis=-1)
        summed = jnp.einsum(
            "hqk,khd->qhd", expos.astype(jnp.bfloat16), part_values, preferred_element_type=jnp.float32
        )
        attended = summed / jnp.transpose(running_total)[:, :, None]
        outputs.append(attended.astype(jnp.bfloat16).reshape(tokens_here, count * HD))
    attended = jnp.concatenate(outputs, axis=1)
    if shared:
        attended = jnp.roll(attended, lax.axis_index("groups") * (width // 2), axis=1)
    return attended


def solution(mesh):
    in_specs = (
        P(("groups", "seq", "row"), "col"),
        P("seq", ("row", "col")),
        P("seq", ("row", "col")),
        P("seq", ("row", "col")),
    )
    out_specs = P(("groups", "seq"), ("row", "col"))
    return jax.shard_map(
        per_device, mesh=mesh, in_specs=in_specs, out_specs=out_specs, check_vma=False
    )
```

```python
import jax
import jax.numpy as jnp
from jax import lax
from jax.sharding import PartitionSpec as P

HD = 128
SPAN = 4


def passed_along(block, axis, distance):
    devices = range(lax.axis_size(axis))
    route = [((i - distance) % len(devices), i) for i in devices]
    return lax.ppermute(block, axis, route)


def line_gather(piece):
    n = lax.axis_size("seq")
    here = lax.axis_index("seq")
    from_right = [piece]
    from_left = [piece]
    for k in range(1, n):
        from_right.append(lax.ppermute(from_right[-1], "seq", [(j, j - 1) for j in range(1, n - k + 1)]))
        from_left.append(lax.ppermute(from_left[-1], "seq", [(j, j + 1) for j in range(k - 1, n - 1)]))
    slots = [piece]
    for m in range(1, n):
        slots.append(jnp.where(here + m < n, from_right[m], from_left[n - m]))
    return jnp.concatenate(slots, axis=0)


def swap_gather(piece, axis, dim):
    if lax.axis_size(axis) != 2:
        return lax.all_gather(piece, axis, axis=dim, tiled=True)
    first = lax.axis_index(axis) == 0
    other = lax.ppermute(piece, axis, [(0, 1), (1, 0)])
    low = jnp.where(first, piece, other)
    high = jnp.where(first, other, piece)
    return jnp.concatenate([low, high], axis=dim)


def full_columns(weight, shared, after=None):
    if not shared:
        return [lax.all_gather(weight, "seq", axis=0, tiled=True)]
    rows, half = weight.shape[0], weight.shape[1] // 2
    group = lax.axis_index("groups")
    own = lax.dynamic_slice_in_dim(weight, group * half, half, axis=1)
    kept = lax.dynamic_slice_in_dim(weight, (1 - group) * half, half, axis=1)
    own = lax.all_gather(own, "seq", axis=0, tiled=True)
    own = jnp.roll(own, -lax.axis_index("seq") * rows, axis=0)
    if after is not None:
        own = lax.optimization_barrier((own, after))[0]
    other = lax.ppermute(own[rows:], "groups", [(0, 1), (1, 0)])
    return [own, jnp.concatenate([kept, other], axis=0)]


def query_columns(weight, after):
    rows, quarter = weight.shape[0], weight.shape[1] // 4
    group = lax.axis_index("groups")
    ordered = jnp.roll(weight, -group * 2 * quarter, axis=1)
    own = lax.all_gather(ordered[:, : 3 * quarter], "seq", axis=0, tiled=True)
    own = jnp.roll(own, -lax.axis_index("seq") * rows, axis=0)
    own = lax.optimization_barrier((own, after))[0]
    other = lax.ppermute(own[rows:, quarter : 2 * quarter], "groups", [(0, 1), (1, 0)])
    return [own, jnp.concatenate([ordered[:, 3 * quarter :], other], axis=0)]


def per_device(acts, w_query, w_key, w_value):
    block = swap_gather(acts, "row", 0)
    block = swap_gather(block, "col", 1)
    tokens_here = block.shape[0]
    width = w_query.shape[1]
    heads_here = width // HD
    shared = lax.axis_size("groups") == 2 and width % (2 * HD) == 0
    if shared:
        block = jnp.roll(block, -lax.axis_index("seq") * w_query.shape[0], axis=1)

    def project(weight, after=None):
        return [
            jnp.dot(block, piece, preferred_element_type=jnp.float32).astype(jnp.bfloat16)
            for piece in full_columns(weight, shared, after)
        ]

    key = jnp.concatenate(project(w_key), axis=1)
    value = jnp.concatenate(project(w_value), axis=1)
    if shared and width % (4 * HD) == 0:
        queries = [
            jnp.dot(block, piece, preferred_element_type=jnp.float32).astype(jnp.bfloat16)
            for piece in query_columns(w_query, key)
        ]
    else:
        queries = project(w_query, key)
    if lax.axis_size("seq") == SPAN:
        seen = jnp.stack([line_gather(key), line_gather(value)])
    else:
        packed = jnp.stack([key, value])
        blocks_seen = [packed]
        current = packed
        for step in range(1, SPAN):
            current = passed_along(current, "seq", 1)
            blocks_seen.append(current)
        seen = jnp.concatenate(blocks_seen, axis=1)
    seen_keys = seen[0].reshape(-1, heads_here, HD)
    seen_values = seen[1].reshape(-1, heads_here, HD)
    scale = 1.0 / jnp.sqrt(jnp.float32(HD))
    outputs = []
    first = 0
    for query in queries:
        count = query.shape[1] // HD
        query = query.reshape(tokens_here, count, HD)
        part_keys = seen_keys[:, first : first + count]
        part_values = seen_values[:, first : first + count]
        first += count
        scores = jnp.einsum("qhd,khd->hqk", query, part_keys, preferred_element_type=jnp.float32) * scale
        largest = scores.max(axis=-1, keepdims=True)
        expos = jnp.exp(scores - largest)
        running_total = jnp.sum(expos, axis=-1)
        summed = jnp.einsum(
            "hqk,khd->qhd", expos.astype(jnp.bfloat16), part_values, preferred_element_type=jnp.float32
        )
        attended = summed / jnp.transpose(running_total)[:, :, None]
        outputs.append(attended.astype(jnp.bfloat16).reshape(tokens_here, count * HD))
    attended = jnp.concatenate(outputs, axis=1)
    if shared:
        attended = jnp.roll(attended, lax.axis_index("groups") * (width // 2), axis=1)
    return attended


def solution(mesh):
    in_specs = (
        P(("groups", "seq", "row"), "col"),
        P("seq", ("row", "col")),
        P("seq", ("row", "col")),
        P("seq", ("row", "col")),
    )
    out_specs = P(("groups", "seq"), ("row", "col"))
    return jax.shard_map(
        per_device, mesh=mesh, in_specs=in_specs, out_specs=out_specs, check_vma=False
    )
```

```python
import jax
import jax.numpy as jnp
from jax import lax
from jax.sharding import PartitionSpec as P

HD = 128
SPAN = 4


def passed_along(block, axis, distance):
    devices = range(lax.axis_size(axis))
    route = [((i - distance) % len(devices), i) for i in devices]
    return lax.ppermute(block, axis, route)


def line_gather(piece, axis=0):
    n = lax.axis_size("seq")
    here = lax.axis_index("seq")
    from_right = [piece]
    from_left = [piece]
    for k in range(1, n):
        from_right.append(lax.ppermute(from_right[-1], "seq", [(j, j - 1) for j in range(1, n - k + 1)]))
        from_left.append(lax.ppermute(from_left[-1], "seq", [(j, j + 1) for j in range(k - 1, n - 1)]))
    slots = [piece]
    for m in range(1, n):
        slots.append(jnp.where(here + m < n, from_right[m], from_left[n - m]))
    return jnp.concatenate(slots, axis=axis)


def swap_gather(piece, axis, dim):
    if lax.axis_size(axis) != 2:
        return lax.all_gather(piece, axis, axis=dim, tiled=True)
    first = lax.axis_index(axis) == 0
    other = lax.ppermute(piece, axis, [(0, 1), (1, 0)])
    low = jnp.where(first, piece, other)
    high = jnp.where(first, other, piece)
    return jnp.concatenate([low, high], axis=dim)


def full_columns(weight, shared, after=None):
    if not shared:
        return [lax.all_gather(weight, "seq", axis=0, tiled=True)]
    rows, half = weight.shape[0], weight.shape[1] // 2
    group = lax.axis_index("groups")
    own = lax.dynamic_slice_in_dim(weight, group * half, half, axis=1)
    kept = lax.dynamic_slice_in_dim(weight, (1 - group) * half, half, axis=1)
    own = lax.all_gather(own, "seq", axis=0, tiled=True)
    own = jnp.roll(own, -lax.axis_index("seq") * rows, axis=0)
    if after is not None:
        own = lax.optimization_barrier((own, after))[0]
    other = lax.ppermute(own[rows:], "groups", [(0, 1), (1, 0)])
    return [own, jnp.concatenate([kept, other], axis=0)]


def per_device(acts, w_query, w_key, w_value):
    block = swap_gather(acts, "row", 0)
    block = swap_gather(block, "col", 1)
    tokens_here = block.shape[0]
    width = w_query.shape[1]
    heads_here = width // HD
    shared = lax.axis_size("groups") == 2 and width % (2 * HD) == 0
    if shared:
        block = jnp.roll(block, -lax.axis_index("seq") * w_query.shape[0], axis=1)

    def project(weight, after=None):
        return [
            jnp.dot(block, piece, preferred_element_type=jnp.float32).astype(jnp.bfloat16)
            for piece in full_columns(weight, shared, after)
        ]

    key = jnp.concatenate(project(w_key), axis=1)
    value = jnp.concatenate(project(w_value), axis=1)
    queries = project(w_query, key)
    if lax.axis_size("seq") == SPAN:
        seen = line_gather(jnp.stack([key, value]), axis=1)
    else:
        packed = jnp.stack([key, value])
        blocks_seen = [packed]
        current = packed
        for step in range(1, SPAN):
            current = passed_along(current, "seq", 1)
            blocks_seen.append(current)
        seen = jnp.concatenate(blocks_seen, axis=1)
    seen_keys = seen[0].reshape(-1, heads_here, HD)
    seen_values = seen[1].reshape(-1, heads_here, HD)
    scale = 1.0 / jnp.sqrt(jnp.float32(HD))
    outputs = []
    first = 0
    for query in queries:
        count = query.shape[1] // HD
        query = query.reshape(tokens_here, count, HD)
        part_keys = seen_keys[:, first : first + count]
        part_values = seen_values[:, first : first + count]
        first += count
        scores = jnp.einsum("qhd,khd->hqk", query, part_keys, preferred_element_type=jnp.float32) * scale
        largest = scores.max(axis=-1, keepdims=True)
        expos = jnp.exp(scores - largest)
        running_total = jnp.sum(expos, axis=-1)
        summed = jnp.einsum(
            "hqk,khd->qhd", expos.astype(jnp.bfloat16), part_values, preferred_element_type=jnp.float32
        )
        attended = summed / jnp.transpose(running_total)[:, :, None]
        outputs.append(attended.astype(jnp.bfloat16).reshape(tokens_here, count * HD))
    attended = jnp.concatenate(outputs, axis=1)
    if shared:
        attended = jnp.roll(attended, lax.axis_index("groups") * (width // 2), axis=1)
    return attended


def solution(mesh):
    in_specs = (
        P(("groups", "seq", "row"), "col"),
        P("seq", ("row", "col")),
        P("seq", ("row", "col")),
        P("seq", ("row", "col")),
    )
    out_specs = P(("groups", "seq"), ("row", "col"))
    return jax.shard_map(
        per_device, mesh=mesh, in_specs=in_specs, out_specs=out_specs, check_vma=False
    )
```

```python
import jax
import jax.numpy as jnp
from jax import lax
from jax.sharding import PartitionSpec as P

HD = 128
SPAN = 4


def passed_along(block, axis, distance):
    devices = range(lax.axis_size(axis))
    route = [((i - distance) % len(devices), i) for i in devices]
    return lax.ppermute(block, axis, route)


def line_gather(piece):
    n = lax.axis_size("seq")
    here = lax.axis_index("seq")
    from_right = [piece]
    from_left = [piece]
    for k in range(1, n):
        from_right.append(lax.ppermute(from_right[-1], "seq", [(j, j - 1) for j in range(1, n - k + 1)]))
        from_left.append(lax.ppermute(from_left[-1], "seq", [(j, j + 1) for j in range(k - 1, n - 1)]))
    slots = [piece]
    for m in range(1, n):
        slots.append(jnp.where(here + m < n, from_right[m], from_left[n - m]))
    return jnp.concatenate(slots, axis=0)


def swap_gather(piece, axis, dim):
    if lax.axis_size(axis) != 2:
        return lax.all_gather(piece, axis, axis=dim, tiled=True)
    first = lax.axis_index(axis) == 0
    other = lax.ppermute(piece, axis, [(0, 1), (1, 0)])
    low = jnp.where(first, piece, other)
    high = jnp.where(first, other, piece)
    return jnp.concatenate([low, high], axis=dim)


def full_columns(weight, shared, after=None):
    if not shared:
        return [lax.all_gather(weight, "seq", axis=0, tiled=True)]
    rows, half = weight.shape[0], weight.shape[1] // 2
    group = lax.axis_index("groups")
    own = lax.dynamic_slice_in_dim(weight, group * half, half, axis=1)
    kept = lax.dynamic_slice_in_dim(weight, (1 - group) * half, half, axis=1)
    own = lax.all_gather(own, "seq", axis=0, tiled=True)
    own = jnp.roll(own, -lax.axis_index("seq") * rows, axis=0)
    if after is not None:
        own = lax.optimization_barrier((own, after))[0]
    other = lax.ppermute(own[rows:], "groups", [(0, 1), (1, 0)])
    return [own, jnp.concatenate([kept, other], axis=0)]


def per_device(acts, w_query, w_key, w_value):
    block = swap_gather(acts, "row", 0)
    block = swap_gather(block, "col", 1)
    tokens_here = block.shape[0]
    width = w_query.shape[1]
    heads_here = width // HD
    shared = lax.axis_size("groups") == 2 and width % (2 * HD) == 0
    if shared:
        block = jnp.roll(block, -lax.axis_index("seq") * w_query.shape[0], axis=1)

    def project(weight, after=None):
        return [
            jnp.dot(block, piece, preferred_element_type=jnp.float32).astype(jnp.bfloat16)
            for piece in full_columns(weight, shared, after)
        ]

    key = jnp.concatenate(project(w_key), axis=1)
    value = jnp.concatenate(project(w_value), axis=1)
    queries = project(w_query, key)
    if lax.axis_size("seq") == SPAN:
        seen = jnp.stack([line_gather(key), line_gather(value)])
    else:
        packed = jnp.stack([key, value])
        blocks_seen = [packed]
        current = packed
        for step in range(1, SPAN):
            current = passed_along(current, "seq", 1)
            blocks_seen.append(current)
        seen = jnp.concatenate(blocks_seen, axis=1)
    seen_keys = seen[0].reshape(-1, heads_here, HD)
    seen_values = seen[1].reshape(-1, heads_here, HD)
    scale = 1.0 / jnp.sqrt(jnp.float32(HD))
    outputs = []
    first = 0
    for query in queries:
        count = query.shape[1] // HD
        query = query.reshape(tokens_here, count, HD)
        part_keys = seen_keys[:, first : first + count]
        part_values = seen_values[:, first : first + count]
        first += count
        scores = jnp.einsum("qhd,khd->hqk", query, part_keys, preferred_element_type=jnp.float32) * scale
        largest = scores.max(axis=-1, keepdims=True)
        expos = jnp.exp(scores - largest)
        running_total = jnp.sum(expos, axis=-1)
        summed = jnp.einsum(
            "hqk,khd->qhd", expos.astype(jnp.bfloat16), part_values, preferred_element_type=jnp.float32
        )
        attended = summed / jnp.transpose(running_total)[:, :, None]
        outputs.append(attended.astype(jnp.bfloat16).reshape(tokens_here, count * HD))
    if shared:
        first_group = lax.axis_index("groups") == 0
        return jnp.where(
            first_group,
            jnp.concatenate(outputs, axis=1),
            jnp.concatenate(outputs[::-1], axis=1),
        )
    return jnp.concatenate(outputs, axis=1)


def solution(mesh):
    in_specs = (
        P(("groups", "seq", "row"), "col"),
        P("seq", ("row", "col")),
        P("seq", ("row", "col")),
        P("seq", ("row", "col")),
    )
    out_specs = P(("groups", "seq"), ("row", "col"))
    return jax.shard_map(
        per_device, mesh=mesh, in_specs=in_specs, out_specs=out_specs, check_vma=False
    )
```

```python
import jax
import jax.numpy as jnp
from jax import lax
from jax.sharding import PartitionSpec as P

HD = 128
SPAN = 4


def passed_along(block, axis, distance):
    devices = range(lax.axis_size(axis))
    route = [((i - distance) % len(devices), i) for i in devices]
    return lax.ppermute(block, axis, route)


def line_gather(piece):
    n = lax.axis_size("seq")
    here = lax.axis_index("seq")
    from_right = [piece]
    from_left = [piece]
    for k in range(1, n):
        from_right.append(lax.ppermute(from_right[-1], "seq", [(j, j - 1) for j in range(1, n - k + 1)]))
        from_left.append(lax.ppermute(from_left[-1], "seq", [(j, j + 1) for j in range(k - 1, n - 1)]))
    slots = [piece]
    for m in range(1, n):
        slots.append(jnp.where(here + m < n, from_right[m], from_left[n - m]))
    return jnp.concatenate(slots, axis=0)


def swap_gather(piece, axis, dim):
    if lax.axis_size(axis) != 2:
        return lax.all_gather(piece, axis, axis=dim, tiled=True)
    first = lax.axis_index(axis) == 0
    other = lax.ppermute(piece, axis, [(0, 1), (1, 0)])
    low = jnp.where(first, piece, other)
    high = jnp.where(first, other, piece)
    return jnp.concatenate([low, high], axis=dim)


def full_columns(weight, shared, after=None):
    if not shared:
        return [lax.all_gather(weight, "seq", axis=0, tiled=True)]
    rows, half = weight.shape[0], weight.shape[1] // 2
    group = lax.axis_index("groups")
    first = group == 0
    own = jnp.where(first, weight[:, :half], weight[:, half:])
    kept = jnp.where(first, weight[:, half:], weight[:, :half])
    own = lax.all_gather(own, "seq", axis=0, tiled=True)
    own = jnp.roll(own, -lax.axis_index("seq") * rows, axis=0)
    if after is not None:
        own = lax.optimization_barrier((own, after))[0]
    other = lax.ppermute(own[rows:], "groups", [(0, 1), (1, 0)])
    return [own, jnp.concatenate([kept, other], axis=0)]


def per_device(acts, w_query, w_key, w_value):
    block = swap_gather(acts, "row", 0)
    block = swap_gather(block, "col", 1)
    tokens_here = block.shape[0]
    width = w_query.shape[1]
    heads_here = width // HD
    shared = lax.axis_size("groups") == 2 and width % (2 * HD) == 0
    if shared:
        block = jnp.roll(block, -lax.axis_index("seq") * w_query.shape[0], axis=1)

    def project(weight, after=None):
        return [
            jnp.dot(block, piece, preferred_element_type=jnp.float32).astype(jnp.bfloat16)
            for piece in full_columns(weight, shared, after)
        ]

    key = jnp.concatenate(project(w_key), axis=1)
    value = jnp.concatenate(project(w_value), axis=1)
    queries = project(w_query, key)
    if lax.axis_size("seq") == SPAN:
        seen = jnp.stack([line_gather(key), line_gather(value)])
    else:
        packed = jnp.stack([key, value])
        blocks_seen = [packed]
        current = packed
        for step in range(1, SPAN):
            current = passed_along(current, "seq", 1)
            blocks_seen.append(current)
        seen = jnp.concatenate(blocks_seen, axis=1)
    seen_keys = seen[0].reshape(-1, heads_here, HD)
    seen_values = seen[1].reshape(-1, heads_here, HD)
    scale = 1.0 / jnp.sqrt(jnp.float32(HD))
    outputs = []
    first = 0
    for query in queries:
        count = query.shape[1] // HD
        query = query.reshape(tokens_here, count, HD)
        part_keys = seen_keys[:, first : first + count]
        part_values = seen_values[:, first : first + count]
        first += count
        scores = jnp.einsum("qhd,khd->hqk", query, part_keys, preferred_element_type=jnp.float32) * scale
        largest = scores.max(axis=-1, keepdims=True)
        expos = jnp.exp(scores - largest)
        running_total = jnp.sum(expos, axis=-1)
        summed = jnp.einsum(
            "hqk,khd->qhd", expos.astype(jnp.bfloat16), part_values, preferred_element_type=jnp.float32
        )
        attended = summed / jnp.transpose(running_total)[:, :, None]
        outputs.append(attended.astype(jnp.bfloat16).reshape(tokens_here, count * HD))
    attended = jnp.concatenate(outputs, axis=1)
    if shared:
        attended = jnp.roll(attended, lax.axis_index("groups") * (width // 2), axis=1)
    return attended


def solution(mesh):
    in_specs = (
        P(("groups", "seq", "row"), "col"),
        P("seq", ("row", "col")),
        P("seq", ("row", "col")),
        P("seq", ("row", "col")),
    )
    out_specs = P(("groups", "seq"), ("row", "col"))
    return jax.shard_map(
        per_device, mesh=mesh, in_specs=in_specs, out_specs=out_specs, check_vma=False
    )
```

```python
import jax
import jax.numpy as jnp
from jax import lax
from jax.sharding import PartitionSpec as P

HD = 128
SPAN = 4


def passed_along(block, axis, distance):
    devices = range(lax.axis_size(axis))
    route = [((i - distance) % len(devices), i) for i in devices]
    return lax.ppermute(block, axis, route)


def line_gather(piece):
    n = lax.axis_size("seq")
    here = lax.axis_index("seq")
    from_right = [piece]
    from_left = [piece]
    for k in range(1, n):
        from_right.append(lax.ppermute(from_right[-1], "seq", [(j, j - 1) for j in range(1, n - k + 1)]))
        from_left.append(lax.ppermute(from_left[-1], "seq", [(j, j + 1) for j in range(k - 1, n - 1)]))
    slots = [piece]
    for m in range(1, n):
        slots.append(jnp.where(here + m < n, from_right[m], from_left[n - m]))
    return jnp.concatenate(slots, axis=0)


def swap_gather(piece, axis, dim):
    if lax.axis_size(axis) != 2:
        return lax.all_gather(piece, axis, axis=dim, tiled=True)
    first = lax.axis_index(axis) == 0
    other = lax.ppermute(piece, axis, [(0, 1), (1, 0)])
    low = jnp.where(first, piece, other)
    high = jnp.where(first, other, piece)
    return jnp.concatenate([low, high], axis=dim)


def full_columns(weight, shared, after=None):
    if not shared:
        return [lax.all_gather(weight, "seq", axis=0, tiled=True)]
    rows, half = weight.shape[0], weight.shape[1] // 2
    group = lax.axis_index("groups")
    first = group == 0
    own = jnp.where(first, weight[:, :half], weight[:, half:])
    kept = jnp.where(first, weight[:, half:], weight[:, :half])
    own = lax.all_gather(own, "seq", axis=0, tiled=True)
    own = jnp.roll(own, -lax.axis_index("seq") * rows, axis=0)
    if after is not None:
        own = lax.optimization_barrier((own, after))[0]
    other = lax.ppermute(own[rows:], "groups", [(0, 1), (1, 0)])
    return [own, (kept, other)]


def per_device(acts, w_query, w_key, w_value):
    block = swap_gather(acts, "row", 0)
    block = swap_gather(block, "col", 1)
    tokens_here = block.shape[0]
    width = w_query.shape[1]
    heads_here = width // HD
    shared = lax.axis_size("groups") == 2 and width % (2 * HD) == 0
    if shared:
        block = jnp.roll(block, -lax.axis_index("seq") * w_query.shape[0], axis=1)

    def product(piece):
        if isinstance(piece, tuple):
            kept, other = piece
            rows = kept.shape[0]
            early = jnp.dot(block[:, :rows], kept, preferred_element_type=jnp.float32)
            return early + jnp.dot(block[:, rows:], other, preferred_element_type=jnp.float32)
        return jnp.dot(block, piece, preferred_element_type=jnp.float32)

    def project(weight, after=None):
        return [product(piece).astype(jnp.bfloat16) for piece in full_columns(weight, shared, after)]

    key = jnp.concatenate(project(w_key), axis=1)
    value = jnp.concatenate(project(w_value), axis=1)
    queries = project(w_query, key)
    if lax.axis_size("seq") == SPAN:
        seen = jnp.stack([line_gather(key), line_gather(value)])
    else:
        packed = jnp.stack([key, value])
        blocks_seen = [packed]
        current = packed
        for step in range(1, SPAN):
            current = passed_along(current, "seq", 1)
            blocks_seen.append(current)
        seen = jnp.concatenate(blocks_seen, axis=1)
    seen_keys = seen[0].reshape(-1, heads_here, HD)
    seen_values = seen[1].reshape(-1, heads_here, HD)
    scale = 1.0 / jnp.sqrt(jnp.float32(HD))
    outputs = []
    first = 0
    for query in queries:
        count = query.shape[1] // HD
        query = query.reshape(tokens_here, count, HD)
        part_keys = seen_keys[:, first : first + count]
        part_values = seen_values[:, first : first + count]
        first += count
        scores = jnp.einsum("qhd,khd->hqk", query, part_keys, preferred_element_type=jnp.float32) * scale
        largest = scores.max(axis=-1, keepdims=True)
        expos = jnp.exp(scores - largest)
        running_total = jnp.sum(expos, axis=-1)
        summed = jnp.einsum(
            "hqk,khd->qhd", expos.astype(jnp.bfloat16), part_values, preferred_element_type=jnp.float32
        )
        attended = summed / jnp.transpose(running_total)[:, :, None]
        outputs.append(attended.astype(jnp.bfloat16).reshape(tokens_here, count * HD))
    if shared:
        first_group = lax.axis_index("groups") == 0
        return jnp.where(
            first_group,
            jnp.concatenate(outputs, axis=1),
            jnp.concatenate(outputs[::-1], axis=1),
        )
    return jnp.concatenate(outputs, axis=1)


def solution(mesh):
    in_specs = (
        P(("groups", "seq", "row"), "col"),
        P("seq", ("row", "col")),
        P("seq", ("row", "col")),
        P("seq", ("row", "col")),
    )
    out_specs = P(("groups", "seq"), ("row", "col"))
    return jax.shard_map(
        per_device, mesh=mesh, in_specs=in_specs, out_specs=out_specs, check_vma=False
    )
```
